32 devices in a mesh: groups: 2 (over y), tile: 4 (over z), dither: 2 (over x), band: 2 (over core).
Axes of the slice: x: 2, y: 2, z: 4, core: 2. Of those that a mesh axis runs over, the one named last changes fastest.
Arguments:
- spectra: bfloat16 [2048, 1024], P(('groups', 'tile'), 'band'), parts along dimension 0, may hold values from -6 to 6
- psf_blocks: bfloat16 [16, 128, 128], replicated, may hold values from -0.5 to 0.5
- observed: bfloat16 [4, 4096, 128], P(('groups', 'dither'), 'tile'), parts along dimension 0, may hold values from -6 to 6
- bad_mask: int32 [4, 4096, 128], P(('groups', 'dither'), 'tile'), parts along dimension 0, may hold values 0 or 1
- trace_tile: int32 [32768, 1], P(('groups', 'tile', 'dither', 'band')), parts along dimension 0, may hold values from 0 to 3; in each aligned block of 1024 rows (0 to 1023, 1024 to 2047, ...) at most 512 rows name the same one
- trace_slot: int32 [32768], P(('groups', 'tile', 'dither', 'band')), parts along dimension 0, may hold values from 0 to 1023
- trace_source: int32 [32768, 1], P(('groups', 'tile', 'dither', 'band')), parts along dimension 0, may hold values from 0 to 255; in each aligned block of 1024 rows (0 to 1023, 1024 to 2047, ...) at most 8 rows name the same one
- trace_block: int32 [32768], P(('groups', 'tile', 'dither', 'band')), parts along dimension 0, may hold values from 0 to 3
- psf_index: int32 [32768], P(('groups', 'tile', 'dither', 'band')), parts along dimension 0, may hold values from 0 to 15
Outputs:
- gradient: float32 [2048, 1024], P(('groups', 'tile', 'dither'), 'band'), parts along dimension 0
- residual: bfloat16 [4, 4096, 128], P(('groups', 'dither'), 'tile'), parts along dimension 0
The draws below stay inside these ranges and needn't reach their ends.
There are 2 independent parts, one for each index of `groups`. The reference program is written for one: setup_inputs(seed, part) draws one part's arguments, and reference() takes and returns one part's arrays. A program takes and returns all parts, laid end to end along the dimension named above; an argument that names none is the same for every part. Nothing has to cross between parts.
Inputs may be any that keep to these rules, and one draw needn't show every extreme that they name: `trace_tile`: among the trace blocks of one sky region, dither and wavelength half, at most 512 name the same tile, and in every draw some tile is named by exactly 512 of them for some such group. `trace_source`: among the trace blocks of one sky region, dither and wavelength half, at most 8 name the same source, and in every draw some source is named by exactly 8 of them for some such group.
All inputs are finite; a program needn't handle non-finite values. No bound on the sum of `bad_mask` on one device may be relied on, other than what follows from the above.
Results may differ from the reference program's by a relative error of at most 0.006.
Values may be sent and summed in bfloat16 or wider, within the bound.
No kernel may reach another device: no remote copies, remote signals or barrier semaphores. Data moves between devices by JAX's collectives and lax.ppermute only.
A program may use at most 64 MiB of HBM per device.

```python
import math
import jax
import jax.numpy as jnp
import numpy as np
from jax import lax

BIN = 128
TRACE = 128
NWAVE = 1024
NPSF = 16
SRC_DEV = 256
ENT_DEV = 1024
SLOTS = 1024
NWB = 8
WB_DEV = 4
TILES = 4
DITHERS = 2
BANDS = 2
SOURCES = 1024
ENTRIES = 16384
CAP = 512
SRC_MOST = 8
N_TILE = 4


def set_ends(values, stream_key, smallest, top_value):
    place = [jax.random.randint(jax.random.fold_in(stream_key, axis), (), 0, length) for axis, length in enumerate(values.shape)]
    longest = values.shape.index(max(values.shape))
    beside = place[:longest] + [(place[longest] + 1) % values.shape[longest]] + place[longest + 1:]
    return values.at[tuple(place)].set(smallest).at[tuple(beside)].set(top_value)


def levels(own_key, extent, cuts, smallest, largest):
    gain = 1.0
    for dim, shards_of in cuts:
        steps = jax.random.uniform(jax.random.fold_in(jax.random.fold_in(own_key, 6), dim), (shards_of,), jnp.float32, smallest / len(cuts), largest / len(cuts))
        gain = gain * jnp.repeat(jnp.exp(steps), extent[dim] // shards_of).reshape((-1,) + (1,) * (len(extent) - 1 - dim))
    return gain


def deal_out(own_key, own, number, rows, count, top, bound, slope):
    sequence = jax.random.permutation(own_key, count)
    packed, usual = portions_of(count, rows * top, bound, slope, True), portions_of(count, rows * top, bound, slope, False)
    places = jnp.arange(count)

    def named(lengths, turn):
        used = int((lengths > 0).sum())
        fixed = max(1, used // 4)
        moved = fixed + (places - fixed + turn * (used - fixed)) % max(1, count - fixed)
        return jnp.zeros((count,), jnp.int32).at[sequence[jnp.where(places < fixed, places, moved)]].set(jnp.asarray(lengths, jnp.int32))

    lengths = jnp.where(number % 4 == 0, named(packed, number // 4), named(usual, number - number // 4 - 1))
    mixed = jax.random.permutation(jax.random.fold_in(own, 3), count)
    source_of, receiver = mixed[0:count // 2 * 2:2], mixed[1:count // 2 * 2:2]
    slack = jnp.minimum(lengths[source_of] - 1, bound - lengths[receiver]) // 2
    slack = jnp.where((source_of == sequence[0]) | (receiver == sequence[0]) | (lengths[receiver] == 0), 0, jnp.maximum(slack, 0))
    moved = jax.random.randint(jax.random.fold_in(own, 4), (count // 2,), 0, 1 << 20) % (slack + 1)
    lengths = lengths.at[source_of].add(-moved).at[receiver].add(moved)
    members = jnp.searchsorted(jnp.cumsum(lengths), jnp.arange(rows * top), side="right").astype(jnp.int32)
    table = members.reshape(top, rows).T
    table = table[jax.random.permutation(jax.random.fold_in(own, 1), rows)]
    turn = jax.random.randint(jax.random.fold_in(own, 2), (rows, 1), 0, top)
    return jnp.take_along_axis(table, (jnp.arange(top)[None, :] + turn) % top, axis=1)


def portions_of(amount, total, limit, slope, full):
    portions = [(1 << 20) // math.isqrt(grade ** slope) + 1 for grade in range(1, amount + 1)]
    largest = limit if full else min(limit, max(-(-total // amount), total * portions[0] // sum(portions)))
    least = 1 if total - largest >= amount - 1 else 0
    holding, rest = [largest] + [least] * (amount - 1), total - largest - least * (amount - 1)
    while rest > 0:
        candidates = [i for i in range(1, amount) if holding[i] < largest] or [i for i in range(1, amount) if holding[i] < limit]
        whole, budget = sum([portions[i] for i in candidates]), rest
        for i in candidates:
            addition = min(limit - holding[i], max(1, budget * portions[i] // whole), rest)
            holding[i] = holding[i] + addition
            rest = rest - addition
    return np.array(holding)


def centred(own_key, dims, deviation, bound, split=(), kind=jnp.bfloat16):
    array = deviation * jax.random.normal(own_key, dims, jnp.float32)
    if split:
        array = array * levels(own_key, dims, split, -0.22, 0.18)
    return jnp.clip(array, -bound, bound).astype(kind)


def setup_inputs(seed: int = 0, part: int = 0) -> dict:
    keys = jax.random.split(jax.random.key(seed), 10)
    part_keys = jax.random.split(jax.random.fold_in(keys[9], part), 10)
    spectra = centred(part_keys[0], (SOURCES, NWAVE), 1.0, 6.0, ((0, 4), (1, 2)))
    psf_blocks = centred(keys[1], (NPSF, BIN, TRACE), BIN ** -0.5, 0.5)
    observed = centred(part_keys[2], (DITHERS, TILES * SLOTS, TRACE), 1.0, 6.0, ((0, 2), (1, 4)))
    bad_mask = set_ends((jax.random.randint(part_keys[3], (DITHERS, TILES * SLOTS, TRACE), 0, 8) < 7).astype(jnp.int32), jax.random.fold_in(part_keys[3], 1), 0, 1)
    trace_tile_keys = jax.random.split(jax.random.fold_in(part_keys[4], 1), ENTRIES // ENT_DEV)
    trace_tile_turns = jax.random.permutation(jax.random.fold_in(part_keys[4], 3), ENTRIES // ENT_DEV)
    trace_tile = jax.vmap(lambda own, number: deal_out(jax.random.fold_in(part_keys[4], 2), own, number, ENT_DEV, N_TILE, 1, CAP, 2))(trace_tile_keys, trace_tile_turns).reshape((ENTRIES, 1))
    trace_slot = set_ends(jax.random.randint(part_keys[5], (ENTRIES,), 0, SLOTS), jax.random.fold_in(part_keys[5], 1), 0, SLOTS - 1).astype(jnp.int32)
    trace_source_keys = jax.random.split(jax.random.fold_in(part_keys[6], 1), ENTRIES // ENT_DEV)
    trace_source_turns = jax.random.permutation(jax.random.fold_in(part_keys[6], 3), ENTRIES // ENT_DEV)
    trace_source = jax.vmap(lambda own, number: deal_out(jax.random.fold_in(part_keys[6], 2), own, number, ENT_DEV, SRC_DEV, 1, SRC_MOST, 1))(trace_source_keys, trace_source_turns).reshape((ENTRIES, 1))
    trace_block = set_ends(jax.random.randint(part_keys[7], (ENTRIES,), 0, WB_DEV), jax.random.fold_in(part_keys[7], 1), 0, WB_DEV - 1).astype(jnp.int32)
    psf_index = set_ends(jax.random.randint(part_keys[8], (ENTRIES,), 0, NPSF), jax.random.fold_in(part_keys[8], 1), 0, NPSF - 1).astype(jnp.int32)
    return {"spectra": spectra, "psf_blocks": psf_blocks, "observed": observed, "bad_mask": bad_mask, "trace_tile": trace_tile, "trace_slot": trace_slot, "trace_source": trace_source, "trace_block": trace_block, "psf_index": psf_index}


def reference(spectra, psf_blocks, observed, bad_mask, trace_tile, trace_slot, trace_source, trace_block, psf_index):
    entry_index = jnp.arange(ENTRIES, dtype=jnp.int32)
    device = entry_index // ENT_DEV
    region = device // (DITHERS * BANDS)
    dither = (device // BANDS) % DITHERS
    band_index = device % BANDS
    source = region * SRC_DEV + trace_source[:, 0].astype(jnp.int32)
    spec_block = band_index * WB_DEV + trace_block.astype(jnp.int32)
    pixel_rows = ((dither * TILES + trace_tile[:, 0].astype(jnp.int32)) * SLOTS + trace_slot.astype(jnp.int32)).astype(jnp.int32)
    spec_rows = (source * NWB + spec_block).astype(jnp.int32)
    stacked = spectra.reshape(SOURCES * NWB, BIN)
    batch_size = math.gcd(ENTRIES, 1024)

    def forward(inputs):
        rows, kinds = inputs
        values = stacked[rows].astype(jnp.float32)
        matrices = psf_blocks[kinds].astype(jnp.float32)
        return jnp.einsum("ek,ekj->ej", values, matrices).astype(jnp.bfloat16)

    traces = lax.map(forward, (spec_rows.reshape(-1, batch_size), psf_index.reshape(-1, batch_size)))
    traces = traces.reshape(ENTRIES, TRACE)
    model_image = jax.ops.segment_sum(traces.astype(jnp.float32), pixel_rows, DITHERS * TILES * SLOTS)
    masks = bad_mask.reshape(-1, TRACE).astype(jnp.float32)
    residual = (masks * (model_image - observed.reshape(-1, TRACE).astype(jnp.float32))).astype(jnp.bfloat16)

    def backward(inputs):
        rows, kinds = inputs
        rows_res = residual[rows].astype(jnp.float32)
        matrices = psf_blocks[kinds].astype(jnp.float32)
        return jnp.einsum("ej,ekj->ek", rows_res, matrices)

    grad_terms = lax.map(backward, (pixel_rows.reshape(-1, batch_size), psf_index.reshape(-1, batch_size)))
    grad_terms = grad_terms.reshape(ENTRIES, BIN)
    gradient = jax.ops.segment_sum(grad_terms, spec_rows, SOURCES * NWB).reshape(SOURCES, NWAVE)
    return gradient, residual.reshape(DITHERS, TILES * SLOTS, TRACE)
```

```python
import jax
import jax.numpy as jnp
from jax import lax
from jax.sharding import PartitionSpec as P


def one_hot_rows(index, width):
    return (index[:, None] == jnp.arange(width, dtype=jnp.int32)[None, :]).astype(jnp.bfloat16)


def select_dot(selector, values, precision=None):
    return jnp.dot(selector, values, preferred_element_type=jnp.float32, precision=precision)


def select_dot_t(selector, values, precision=None):
    return lax.dot_general(
        selector,
        values,
        (((0,), (0,)), ((), ())),
        preferred_element_type=jnp.float32,
        precision=precision,
    )


def spread_by_kind(values, kinds, table_count):
    chosen = kinds[:, None, None] == jnp.arange(table_count, dtype=jnp.int32)[None, :, None]
    spread = jnp.where(chosen, values[:, None, :], jnp.zeros((), values.dtype))
    return spread.reshape(values.shape[0], table_count * values.shape[1])


def swap_add(value, axis):
    count = lax.axis_size(axis)
    if count == 2:
        return value + lax.ppermute(value, axis, [(0, 1), (1, 0)])
    return lax.psum(value, axis)


def per_device(
    spectra,
    psf_blocks,
    observed,
    bad_mask,
    trace_tile,
    trace_slot,
    trace_source,
    trace_block,
    psf_index,
):
    tile_count = lax.axis_size("tile")
    dither_count = lax.axis_size("dither")
    entry_count = trace_slot.shape[0]
    capacity = 2 * entry_count // tile_count
    table_count, bin_count, pixel_count = psf_blocks.shape
    source_count = spectra.shape[0]
    block_count = spectra.shape[1] // bin_count
    row_count = source_count * block_count
    slot_count = observed.shape[1]
    send_count = tile_count * capacity

    target = trace_tile[:, 0]
    kinds = psf_index
    spec_rows = trace_source[:, 0] * block_count + trace_block
    member = (target[:, None] == jnp.arange(tile_count, dtype=jnp.int32)[None, :]).astype(jnp.int32)
    position = jnp.sum((jnp.cumsum(member, axis=0) - 1) * member, axis=1)
    dest = target * capacity + position

    gather_spec = one_hot_rows(spec_rows, row_count)
    spec_values = select_dot(gather_spec, spectra.reshape(row_count, bin_count)).astype(jnp.bfloat16)
    psf_flat = psf_blocks.reshape(table_count * bin_count, pixel_count)
    traces = select_dot(spread_by_kind(spec_values, kinds, table_count), psf_flat).astype(jnp.bfloat16)
    place = one_hot_rows(dest, send_count)
    send_traces = select_dot_t(place, traces).astype(jnp.bfloat16)
    slot_parts = jnp.stack([trace_slot // 256, trace_slot % 256], axis=1).astype(jnp.bfloat16)
    send_slots = select_dot_t(place, slot_parts).astype(jnp.bfloat16)
    code_rows = -(-2 * capacity // pixel_count)
    send_slots = send_slots.reshape(tile_count, 2 * capacity)
    send_slots = jnp.pad(send_slots, ((0, 0), (0, code_rows * pixel_count - 2 * capacity)))
    send = jnp.concatenate(
        [
            send_traces.reshape(tile_count, capacity, pixel_count),
            send_slots.reshape(tile_count, code_rows, pixel_count),
        ],
        axis=1,
    )
    got = lax.all_to_all(send, "tile", split_axis=0, concat_axis=0, tiled=True)
    got_traces = got[:, :capacity].reshape(send_count, pixel_count)
    got_codes = got[:, capacity:].reshape(tile_count, code_rows * pixel_count)[:, : 2 * capacity]
    got_codes = got_codes.astype(jnp.int32).reshape(send_count, 2)
    got_slots = got_codes[:, 0] * 256 + got_codes[:, 1]

    at_slot = one_hot_rows(got_slots, slot_count)
    partial_value = select_dot_t(at_slot, got_traces)
    model_image = swap_add(partial_value, "band")
    residual = (
        bad_mask[0].astype(jnp.float32) * (model_image - observed[0].astype(jnp.float32))
    ).astype(jnp.bfloat16)

    under_rows = select_dot(at_slot, residual).astype(jnp.bfloat16)
    returned = lax.all_to_all(
        under_rows.reshape(tile_count, capacity, pixel_count),
        "tile",
        split_axis=0,
        concat_axis=0,
        tiled=True,
    )
    entry_rows = select_dot(place, returned.reshape(send_count, pixel_count)).astype(jnp.bfloat16)
    back_table = psf_blocks.transpose(0, 2, 1).reshape(table_count * pixel_count, bin_count)
    terms = select_dot(spread_by_kind(entry_rows, kinds, table_count), back_table)
    local_grad = select_dot_t(gather_spec, terms, precision=lax.Precision.HIGHEST)
    local_grad = local_grad.reshape(source_count, block_count * bin_count)

    if dither_count == 2:
        dither = lax.axis_index("dither")
        halves = local_grad.reshape(2, source_count // 2, block_count * bin_count)
        mine = jnp.where(dither == 0, halves[0], halves[1])
        theirs = jnp.where(dither == 0, halves[1], halves[0])
        gradient = mine + lax.ppermute(theirs, "dither", [(0, 1), (1, 0)])
    else:
        gradient = lax.psum_scatter(local_grad, "dither", scatter_dimension=0, tiled=True)
    return (gradient, residual[None])


def solution(mesh):
    in_specs = (
        P(("groups", "tile"), "band"),
        P(),
        P(("groups", "dither"), "tile", None),
        P(("groups", "dither"), "tile", None),
        P(("groups", "tile", "dither", "band"), None),
        P(("groups", "tile", "dither", "band")),
        P(("groups", "tile", "dither", "band"), None),
        P(("groups", "tile", "dither", "band")),
        P(("groups", "tile", "dither", "band")),
    )
    out_specs = (P(("groups", "tile", "dither"), "band"), P(("groups", "dither"), "tile", None))
    return jax.shard_map(
        per_device, mesh=mesh, in_specs=in_specs, out_specs=out_specs, check_vma=False
    )
```

```python
import jax
import jax.numpy as jnp
from jax import lax
from jax.sharding import PartitionSpec as P


def one_hot_rows(index, width):
    return (index[:, None] == jnp.arange(width, dtype=jnp.int32)[None, :]).astype(jnp.bfloat16)


def select_dot(selector, values, precision=None):
    return jnp.dot(selector, values, preferred_element_type=jnp.float32, precision=precision)


def select_dot_t(selector, values, precision=None):
    return lax.dot_general(
        selector,
        values,
        (((0,), (0,)), ((), ())),
        preferred_element_type=jnp.float32,
        precision=precision,
    )


def spread_by_kind(values, kinds, table_count):
    chosen = kinds[:, None, None] == jnp.arange(table_count, dtype=jnp.int32)[None, :, None]
    spread = jnp.where(chosen, values[:, None, :], jnp.zeros((), values.dtype))
    return spread.reshape(values.shape[0], table_count * values.shape[1])


def swap_add(value, axis):
    count = lax.axis_size(axis)
    if count == 2:
        return value + lax.ppermute(value, axis, [(0, 1), (1, 0)])
    return lax.psum(value, axis)


def exchange(blocks, axis, direction):
    count = lax.axis_size(axis)
    moved = [blocks[0]]
    for step in range(1, count):
        pairs = [(j, (j + direction * step) % count) for j in range(count)]
        moved.append(lax.ppermute(blocks[step], axis, pairs))
    return jnp.stack(moved)


def per_device(
    spectra,
    psf_blocks,
    observed,
    bad_mask,
    trace_tile,
    trace_slot,
    trace_source,
    trace_block,
    psf_index,
):
    tile_count = lax.axis_size("tile")
    dither_count = lax.axis_size("dither")
    entry_count = trace_slot.shape[0]
    capacity = 2 * entry_count // tile_count
    table_count, bin_count, pixel_count = psf_blocks.shape
    source_count = spectra.shape[0]
    block_count = spectra.shape[1] // bin_count
    row_count = source_count * block_count
    slot_count = observed.shape[1]
    send_count = tile_count * capacity

    target = trace_tile[:, 0]
    kinds = psf_index
    spec_rows = trace_source[:, 0] * block_count + trace_block
    member = (target[:, None] == jnp.arange(tile_count, dtype=jnp.int32)[None, :]).astype(jnp.int32)
    position = jnp.sum((jnp.cumsum(member, axis=0) - 1) * member, axis=1)
    shift = (target - lax.axis_index("tile")) % tile_count
    dest = shift * capacity + position

    gather_spec = one_hot_rows(spec_rows, row_count)
    spec_values = select_dot(gather_spec, spectra.reshape(row_count, bin_count)).astype(jnp.bfloat16)
    psf_flat = psf_blocks.reshape(table_count * bin_count, pixel_count)
    traces = select_dot(spread_by_kind(spec_values, kinds, table_count), psf_flat).astype(jnp.bfloat16)
    place = one_hot_rows(dest, send_count)
    send_traces = select_dot_t(place, traces).astype(jnp.bfloat16)
    slot_parts = jnp.stack([trace_slot // 256, trace_slot % 256], axis=1).astype(jnp.bfloat16)
    send_slots = select_dot_t(place, slot_parts).astype(jnp.bfloat16)
    code_rows = -(-2 * capacity // pixel_count)
    send_slots = send_slots.reshape(tile_count, 2 * capacity)
    send_slots = jnp.pad(send_slots, ((0, 0), (0, code_rows * pixel_count - 2 * capacity)))
    send = jnp.concatenate(
        [
            send_traces.reshape(tile_count, capacity, pixel_count),
            send_slots.reshape(tile_count, code_rows, pixel_count),
        ],
        axis=1,
    )
    got = exchange(send, "tile", 1)
    got_traces = got[:, :capacity].reshape(send_count, pixel_count)
    got_codes = got[:, capacity:].reshape(tile_count, code_rows * pixel_count)[:, : 2 * capacity]
    got_codes = got_codes.astype(jnp.int32).reshape(send_count, 2)
    got_slots = got_codes[:, 0] * 256 + got_codes[:, 1]

    at_slot = one_hot_rows(got_slots, slot_count)
    partial_value = select_dot_t(at_slot, got_traces)
    model_image = swap_add(partial_value, "band")
    residual = (
        bad_mask[0].astype(jnp.float32) * (model_image - observed[0].astype(jnp.float32))
    ).astype(jnp.bfloat16)

    under_rows = select_dot(at_slot, residual).astype(jnp.bfloat16)
    returned = exchange(under_rows.reshape(tile_count, capacity, pixel_count), "tile", -1)
    entry_rows = select_dot(place, returned.reshape(send_count, pixel_count)).astype(jnp.bfloat16)
    back_table = psf_blocks.transpose(0, 2, 1).reshape(table_count * pixel_count, bin_count)
    terms = select_dot(spread_by_kind(entry_rows, kinds, table_count), back_table)
    terms_hi = terms.astype(jnp.bfloat16)
    terms_lo = (terms - terms_hi.astype(jnp.float32)).astype(jnp.bfloat16)
    local_grad = select_dot_t(gather_spec, terms_hi) + select_dot_t(gather_spec, terms_lo)
    local_grad = local_grad.reshape(source_count, block_count * bin_count)

    if dither_count == 2:
        dither = lax.axis_index("dither")
        halves = local_grad.reshape(2, source_count // 2, block_count * bin_count)
        mine = jnp.where(dither == 0, halves[0], halves[1])
        theirs = jnp.where(dither == 0, halves[1], halves[0])
        gradient = mine + lax.ppermute(theirs, "dither", [(0, 1), (1, 0)])
    else:
        gradient = lax.psum_scatter(local_grad, "dither", scatter_dimension=0, tiled=True)
    return (gradient, residual[None])


def solution(mesh):
    in_specs = (
        P(("groups", "tile"), "band"),
        P(),
        P(("groups", "dither"), "tile", None),
        P(("groups", "dither"), "tile", None),
        P(("groups", "tile", "dither", "band"), None),
        P(("groups", "tile", "dither", "band")),
        P(("groups", "tile", "dither", "band"), None),
        P(("groups", "tile", "dither", "band")),
        P(("groups", "tile", "dither", "band")),
    )
    out_specs = (P(("groups", "tile", "dither"), "band"), P(("groups", "dither"), "tile", None))
    return jax.shard_map(
        per_device, mesh=mesh, in_specs=in_specs, out_specs=out_specs, check_vma=False
    )
```

```python
import jax
import jax.numpy as jnp
from jax import lax
from jax.sharding import PartitionSpec as P


def one_hot_rows(index, width):
    return (index[:, None] == jnp.arange(width, dtype=jnp.int32)[None, :]).astype(jnp.bfloat16)


def select_dot(selector, values, precision=None):
    return jnp.dot(selector, values, preferred_element_type=jnp.float32, precision=precision)


def select_dot_t(selector, values, precision=None):
    return lax.dot_general(
        selector,
        values,
        (((0,), (0,)), ((), ())),
        preferred_element_type=jnp.float32,
        precision=precision,
    )


def spread_by_kind(values, kinds, table_count):
    chosen = kinds[:, None, None] == jnp.arange(table_count, dtype=jnp.int32)[None, :, None]
    spread = jnp.where(chosen, values[:, None, :], jnp.zeros((), values.dtype))
    return spread.reshape(values.shape[0], table_count * values.shape[1])


def swap_add(value, axis):
    count = lax.axis_size(axis)
    if count == 2:
        return value + lax.ppermute(value, axis, [(0, 1), (1, 0)])
    return lax.psum(value, axis)


def exchange(blocks, axis, direction):
    count = lax.axis_size(axis)
    moved = [blocks[0]]
    for step in range(1, count):
        pairs = [(j, (j + direction * step) % count) for j in range(count)]
        moved.append(lax.ppermute(blocks[step], axis, pairs))
    return jnp.stack(moved)


def per_device(
    spectra,
    psf_blocks,
    observed,
    bad_mask,
    trace_tile,
    trace_slot,
    trace_source,
    trace_block,
    psf_index,
):
    tile_count = lax.axis_size("tile")
    dither_count = lax.axis_size("dither")
    entry_count = trace_slot.shape[0]
    capacity = 2 * entry_count // tile_count
    table_count, bin_count, pixel_count = psf_blocks.shape
    source_count = spectra.shape[0]
    block_count = spectra.shape[1] // bin_count
    row_count = source_count * block_count
    slot_count = observed.shape[1]
    send_count = tile_count * capacity

    target = trace_tile[:, 0]
    kinds = psf_index
    spec_rows = trace_source[:, 0] * block_count + trace_block
    member = one_hot_rows(target, tile_count)
    entry_ids = jnp.arange(entry_count, dtype=jnp.int32)
    up_to = (entry_ids[None, :] <= entry_ids[:, None]).astype(jnp.bfloat16)
    running = select_dot(up_to, member)
    position = jnp.sum((running - 1.0) * member.astype(jnp.float32), axis=1).astype(jnp.int32)
    shift = (target - lax.axis_index("tile")) % tile_count
    dest = shift * capacity + position

    gather_spec = one_hot_rows(spec_rows, row_count)
    spec_values = select_dot(gather_spec, spectra.reshape(row_count, bin_count)).astype(jnp.bfloat16)
    psf_flat = psf_blocks.reshape(table_count * bin_count, pixel_count)
    traces = select_dot(spread_by_kind(spec_values, kinds, table_count), psf_flat).astype(jnp.bfloat16)
    place = one_hot_rows(dest, send_count)
    send_traces = select_dot_t(place, traces).astype(jnp.bfloat16)
    slot_parts = jnp.stack([trace_slot // 256, trace_slot % 256], axis=1).astype(jnp.bfloat16)
    send_slots = select_dot_t(place, slot_parts).astype(jnp.bfloat16)
    code_rows = -(-2 * capacity // pixel_count)
    send_slots = send_slots.reshape(tile_count, 2 * capacity)
    send_slots = jnp.pad(send_slots, ((0, 0), (0, code_rows * pixel_count - 2 * capacity)))
    send = jnp.concatenate(
        [
            send_traces.reshape(tile_count, capacity, pixel_count),
            send_slots.reshape(tile_count, code_rows, pixel_count),
        ],
        axis=1,
    )
    got = exchange(send, "tile", 1)
    got_traces = got[:, :capacity].reshape(send_count, pixel_count)
    got_codes = got[:, capacity:].reshape(tile_count, code_rows * pixel_count)[:, : 2 * capacity]
    got_codes = got_codes.astype(jnp.int32).reshape(send_count, 2)
    got_slots = got_codes[:, 0] * 256 + got_codes[:, 1]

    at_slot = one_hot_rows(got_slots, slot_count)
    partial_value = select_dot_t(at_slot, got_traces)
    model_image = swap_add(partial_value, "band")
    residual = (
        bad_mask[0].astype(jnp.float32) * (model_image - observed[0].astype(jnp.float32))
    ).astype(jnp.bfloat16)

    under_rows = select_dot(at_slot, residual).astype(jnp.bfloat16)
    returned = exchange(under_rows.reshape(tile_count, capacity, pixel_count), "tile", -1)
    entry_rows = select_dot(place, returned.reshape(send_count, pixel_count)).astype(jnp.bfloat16)
    back_table = psf_blocks.transpose(0, 2, 1).reshape(table_count * pixel_count, bin_count)
    terms = select_dot(spread_by_kind(entry_rows, kinds, table_count), back_table)
    terms = terms.astype(jnp.bfloat16)

    if dither_count == 2:
        dither = lax.axis_index("dither")
        half_rows = row_count // 2
        own_start = dither * half_rows
        their_rows = one_hot_rows(spec_rows - (half_rows - own_start), half_rows)
        own_rows = one_hot_rows(spec_rows - own_start, half_rows)
        theirs = select_dot_t(their_rows, terms).reshape(source_count // 2, block_count * bin_count)
        sent = lax.ppermute(theirs, "dither", [(0, 1), (1, 0)])
        mine = select_dot_t(own_rows, terms).reshape(source_count // 2, block_count * bin_count)
        gradient = mine + sent
    else:
        local_grad = select_dot_t(gather_spec, terms)
        local_grad = local_grad.reshape(source_count, block_count * bin_count)
        gradient = lax.psum_scatter(local_grad, "dither", scatter_dimension=0, tiled=True)
    return (gradient, residual[None])


def solution(mesh):
    in_specs = (
        P(("groups", "tile"), "band"),
        P(),
        P(("groups", "dither"), "tile", None),
        P(("groups", "dither"), "tile", None),
        P(("groups", "tile", "dither", "band"), None),
        P(("groups", "tile", "dither", "band")),
        P(("groups", "tile", "dither", "band"), None),
        P(("groups", "tile", "dither", "band")),
        P(("groups", "tile", "dither", "band")),
    )
    out_specs = (P(("groups", "tile", "dither"), "band"), P(("groups", "dither"), "tile", None))
    return jax.shard_map(
        per_device, mesh=mesh, in_specs=in_specs, out_specs=out_specs, check_vma=False
    )
```

```python
import jax
import jax.numpy as jnp
from jax import lax
from jax.sharding import PartitionSpec as P


def one_hot_rows(index, width):
    return (index[:, None] == jnp.arange(width, dtype=jnp.int32)[None, :]).astype(jnp.bfloat16)


def select_dot(selector, values, precision=None):
    return jnp.dot(selector, values, preferred_element_type=jnp.float32, precision=precision)


def select_dot_t(selector, values, precision=None):
    return lax.dot_general(
        selector,
        values,
        (((0,), (0,)), ((), ())),
        preferred_element_type=jnp.float32,
        precision=precision,
    )


def spread_by_kind(values, kinds, table_count):
    chosen = kinds[:, None, None] == jnp.arange(table_count, dtype=jnp.int32)[None, :, None]
    spread = jnp.where(chosen, values[:, None, :], jnp.zeros((), values.dtype))
    return spread.reshape(values.shape[0], table_count * values.shape[1])


def swap_add(value, axis):
    count = lax.axis_size(axis)
    if count == 2:
        return value + lax.ppermute(value, axis, [(0, 1), (1, 0)])
    return lax.psum(value, axis)


def exchange(blocks, axis, direction):
    count = lax.axis_size(axis)
    moved = [blocks[0]]
    for step in range(1, count):
        pairs = [(j, (j + direction * step) % count) for j in range(count)]
        moved.append(lax.ppermute(blocks[step], axis, pairs))
    return moved


def per_device(
    spectra,
    psf_blocks,
    observed,
    bad_mask,
    trace_tile,
    trace_slot,
    trace_source,
    trace_block,
    psf_index,
):
    tile_count = lax.axis_size("tile")
    dither_count = lax.axis_size("dither")
    entry_count = trace_slot.shape[0]
    capacity = 2 * entry_count // tile_count
    table_count, bin_count, pixel_count = psf_blocks.shape
    source_count = spectra.shape[0]
    block_count = spectra.shape[1] // bin_count
    row_count = source_count * block_count
    slot_count = observed.shape[1]
    send_count = tile_count * capacity

    target = trace_tile[:, 0]
    kinds = psf_index
    spec_rows = trace_source[:, 0] * block_count + trace_block
    member = one_hot_rows(target, tile_count)
    entry_ids = jnp.arange(entry_count, dtype=jnp.int32)
    up_to = (entry_ids[None, :] <= entry_ids[:, None]).astype(jnp.bfloat16)
    running = select_dot(up_to, member)
    position = jnp.sum((running - 1.0) * member.astype(jnp.float32), axis=1).astype(jnp.int32)
    shift = (target - lax.axis_index("tile")) % tile_count
    dest = shift * capacity + position

    gather_spec = one_hot_rows(spec_rows, row_count)
    spec_values = select_dot(gather_spec, spectra.reshape(row_count, bin_count)).astype(jnp.bfloat16)
    psf_flat = psf_blocks.reshape(table_count * bin_count, pixel_count)
    traces = select_dot(spread_by_kind(spec_values, kinds, table_count), psf_flat).astype(jnp.bfloat16)
    slot_parts = jnp.stack([trace_slot // 256, trace_slot % 256], axis=1).astype(jnp.bfloat16)
    code_rows = -(-2 * capacity // pixel_count)
    places = [one_hot_rows(dest - step * capacity, capacity) for step in range(tile_count)]
    send = []
    for step in range(tile_count):
        codes = select_dot_t(slot_parts, places[step]).astype(jnp.bfloat16).reshape(2 * capacity)
        codes = jnp.pad(codes, (0, code_rows * pixel_count - 2 * capacity))
        block = select_dot_t(places[step], traces).astype(jnp.bfloat16)
        send.append(jnp.concatenate([block, codes.reshape(code_rows, pixel_count)], axis=0))
    got = exchange(send, "tile", 1)
    got_traces = [block[:capacity] for block in got]
    got_slots = []
    for block in got:
        codes = block[capacity:].reshape(code_rows * pixel_count)[: 2 * capacity]
        codes = codes.astype(jnp.int32).reshape(2, capacity)
        got_slots.append(codes[0] * 256 + codes[1])

    at_slot = [one_hot_rows(slots, slot_count) for slots in got_slots]
    partial_value = sum(select_dot_t(a, b) for a, b in zip(at_slot, got_traces))
    model_image = swap_add(partial_value, "band")
    residual = (
        bad_mask[0].astype(jnp.float32) * (model_image - observed[0].astype(jnp.float32))
    ).astype(jnp.bfloat16)

    under_rows = [select_dot(a, residual).astype(jnp.bfloat16) for a in at_slot]
    returned = exchange(under_rows, "tile", -1)
    entry_rows = sum(select_dot(p, r) for p, r in zip(places, returned)).astype(jnp.bfloat16)
    back_table = psf_blocks.transpose(0, 2, 1).reshape(table_count * pixel_count, bin_count)
    terms = select_dot(spread_by_kind(entry_rows, kinds, table_count), back_table)
    terms = terms.astype(jnp.bfloat16)

    if dither_count == 2:
        dither = lax.axis_index("dither")
        half_rows = row_count // 2
        own_start = dither * half_rows
        their_rows = one_hot_rows(spec_rows - (half_rows - own_start), half_rows)
        own_rows = one_hot_rows(spec_rows - own_start, half_rows)
        theirs = select_dot_t(their_rows, terms).reshape(source_count // 2, block_count * bin_count)
        sent = lax.ppermute(theirs.astype(jnp.bfloat16), "dither", [(0, 1), (1, 0)])
        mine = select_dot_t(own_rows, terms).reshape(source_count // 2, block_count * bin_count)
        gradient = mine + sent.astype(jnp.float32)
    else:
        local_grad = select_dot_t(gather_spec, terms)
        local_grad = local_grad.reshape(source_count, block_count * bin_count)
        gradient = lax.psum_scatter(local_grad, "dither", scatter_dimension=0, tiled=True)
    return (gradient, residual[None])


def solution(mesh):
    in_specs = (
        P(("groups", "tile"), "band"),
        P(),
        P(("groups", "dither"), "tile", None),
        P(("groups", "dither"), "tile", None),
        P(("groups", "tile", "dither", "band"), None),
        P(("groups", "tile", "dither", "band")),
        P(("groups", "tile", "dither", "band"), None),
        P(("groups", "tile", "dither", "band")),
        P(("groups", "tile", "dither", "band")),
    )
    out_specs = (P(("groups", "tile", "dither"), "band"), P(("groups", "dither"), "tile", None))
    return jax.shard_map(
        per_device, mesh=mesh, in_specs=in_specs, out_specs=out_specs, check_vma=False
    )
```

```python
import math

import jax
import jax.numpy as jnp
from jax import lax
from jax.sharding import PartitionSpec as P


def one_hot_rows(index, width):
    return (index[:, None] == jnp.arange(width, dtype=jnp.int32)[None, :]).astype(jnp.bfloat16)


def select_dot(selector, values, precision=None):
    return jnp.dot(selector, values, preferred_element_type=jnp.float32, precision=precision)


def select_dot_t(selector, values, precision=None):
    return lax.dot_general(
        selector,
        values,
        (((0,), (0,)), ((), ())),
        preferred_element_type=jnp.float32,
        precision=precision,
    )


def spread_by_kind(values, kinds, table_count):
    chosen = kinds[:, None, None] == jnp.arange(table_count, dtype=jnp.int32)[None, :, None]
    spread = jnp.where(chosen, values[:, None, :], jnp.zeros((), values.dtype))
    return spread.reshape(values.shape[0], table_count * values.shape[1])


def swap_add(value, axis):
    count = lax.axis_size(axis)
    if count == 2:
        return value + lax.ppermute(value, axis, [(0, 1), (1, 0)])
    return lax.psum(value, axis)


def exchange(blocks, axis, direction):
    count = lax.axis_size(axis)
    moved = [blocks[0]]
    for step in range(1, count):
        pairs = [(j, (j + direction * step) % count) for j in range(count)]
        moved.append(lax.ppermute(blocks[step], axis, pairs))
    return moved


def per_device(
    spectra,
    psf_blocks,
    observed,
    bad_mask,
    trace_tile,
    trace_slot,
    trace_source,
    trace_block,
    psf_index,
):
    tile_count = lax.axis_size("tile")
    dither_count = lax.axis_size("dither")
    entry_count = trace_slot.shape[0]
    capacity = 2 * entry_count // tile_count
    table_count, bin_count, pixel_count = psf_blocks.shape
    source_count = spectra.shape[0]
    block_count = spectra.shape[1] // bin_count
    row_count = source_count * block_count
    slot_count = observed.shape[1]
    send_count = tile_count * capacity

    target = trace_tile[:, 0]
    kinds = psf_index
    spec_rows = trace_source[:, 0] * block_count + trace_block
    member = one_hot_rows(target, tile_count)
    chunk = math.gcd(entry_count, 128)
    chunk_ids = jnp.arange(chunk, dtype=jnp.int32)
    up_to = (chunk_ids[None, :] <= chunk_ids[:, None]).astype(jnp.bfloat16)
    within = jnp.einsum(
        "ij,cjt->cit",
        up_to,
        member.reshape(entry_count // chunk, chunk, tile_count),
        preferred_element_type=jnp.float32,
    )
    totals = within[:, -1, :]
    running = (within + (jnp.cumsum(totals, axis=0) - totals)[:, None, :]).reshape(entry_count, tile_count)
    position = jnp.sum((running - 1.0) * member.astype(jnp.float32), axis=1).astype(jnp.int32)
    shift = (target - lax.axis_index("tile")) % tile_count
    dest = shift * capacity + position

    gather_spec = one_hot_rows(spec_rows, row_count)
    spec_values = select_dot(gather_spec, spectra.reshape(row_count, bin_count)).astype(jnp.bfloat16)
    psf_flat = psf_blocks.reshape(table_count * bin_count, pixel_count)
    traces = select_dot(spread_by_kind(spec_values, kinds, table_count), psf_flat).astype(jnp.bfloat16)
    slot_parts = jnp.stack([trace_slot // 256, trace_slot % 256], axis=1).astype(jnp.bfloat16)
    code_rows = -(-2 * capacity // pixel_count)
    places = [one_hot_rows(dest - step * capacity, capacity) for step in range(tile_count)]
    with_codes = jnp.concatenate([traces, slot_parts], axis=1)
    send = []
    for step in range(tile_count):
        placed = select_dot_t(places[step], with_codes).astype(jnp.bfloat16)
        codes = placed[:, pixel_count:].T.reshape(2 * capacity)
        codes = jnp.pad(codes, (0, code_rows * pixel_count - 2 * capacity))
        send.append(
            jnp.concatenate([placed[:, :pixel_count], codes.reshape(code_rows, pixel_count)], axis=0)
        )
    got = exchange(send, "tile", 1)
    got_traces = [block[:capacity] for block in got]
    got_slots = []
    for block in got:
        codes = block[capacity:].reshape(code_rows * pixel_count)[: 2 * capacity]
        codes = codes.astype(jnp.int32).reshape(2, capacity)
        got_slots.append(codes[0] * 256 + codes[1])

    at_slot = [one_hot_rows(slots, slot_count) for slots in got_slots]
    partial_value = sum(select_dot_t(a, b) for a, b in zip(at_slot, got_traces))
    model_image = swap_add(partial_value, "band")
    residual = (
        bad_mask[0].astype(jnp.float32) * (model_image - observed[0].astype(jnp.float32))
    ).astype(jnp.bfloat16)

    under_rows = [select_dot(a, residual).astype(jnp.bfloat16) for a in at_slot]
    returned = exchange(under_rows, "tile", -1)
    entry_rows = sum(select_dot(p, r) for p, r in zip(places, returned)).astype(jnp.bfloat16)
    back_table = psf_blocks.transpose(0, 2, 1).reshape(table_count * pixel_count, bin_count)
    terms = select_dot(spread_by_kind(entry_rows, kinds, table_count), back_table)
    terms = terms.astype(jnp.bfloat16)

    if dither_count == 2:
        dither = lax.axis_index("dither")
        half_rows = row_count // 2
        own_start = dither * half_rows
        their_rows = one_hot_rows(spec_rows - (half_rows - own_start), half_rows)
        own_rows = one_hot_rows(spec_rows - own_start, half_rows)
        theirs = select_dot_t(their_rows, terms).reshape(source_count // 2, block_count * bin_count)
        sent = lax.ppermute(theirs.astype(jnp.bfloat16), "dither", [(0, 1), (1, 0)])
        mine = select_dot_t(own_rows, terms).reshape(source_count // 2, block_count * bin_count)
        gradient = mine + sent.astype(jnp.float32)
    else:
        local_grad = select_dot_t(gather_spec, terms)
        local_grad = local_grad.reshape(source_count, block_count * bin_count)
        gradient = lax.psum_scatter(local_grad, "dither", scatter_dimension=0, tiled=True)
    return (gradient, residual[None])


def solution(mesh):
    in_specs = (
        P(("groups", "tile"), "band"),
        P(),
        P(("groups", "dither"), "tile", None),
        P(("groups", "dither"), "tile", None),
        P(("groups", "tile", "dither", "band"), None),
        P(("groups", "tile", "dither", "band")),
        P(("groups", "tile", "dither", "band"), None),
        P(("groups", "tile", "dither", "band")),
        P(("groups", "tile", "dither", "band")),
    )
    out_specs = (P(("groups", "tile", "dither"), "band"), P(("groups", "dither"), "tile", None))
    return jax.shard_map(
        per_device, mesh=mesh, in_specs=in_specs, out_specs=out_specs, check_vma=False
    )
```

```python
import jax
import jax.numpy as jnp
from jax import lax
from jax.sharding import PartitionSpec as P


def one_hot_rows(index, width):
    return (index[:, None] == jnp.arange(width, dtype=jnp.int32)[None, :]).astype(jnp.bfloat16)


def select_dot(selector, values, precision=None):
    return jnp.dot(selector, values, preferred_element_type=jnp.float32, precision=precision)


def select_dot_t(selector, values, precision=None):
    return lax.dot_general(
        selector,
        values,
        (((0,), (0,)), ((), ())),
        preferred_element_type=jnp.float32,
        precision=precision,
    )


def spread_by_kind(values, kinds, table_count):
    chosen = kinds[:, None, None] == jnp.arange(table_count, dtype=jnp.int32)[None, :, None]
    spread = jnp.where(chosen, values[:, None, :], jnp.zeros((), values.dtype))
    return spread.reshape(values.shape[0], table_count * values.shape[1])


def swap_add(value, axis):
    count = lax.axis_size(axis)
    if count == 2:
        return value + lax.ppermute(value, axis, [(0, 1), (1, 0)])
    return lax.psum(value, axis)


def exchange(blocks, axis, direction):
    count = lax.axis_size(axis)
    moved = [blocks[0]]
    for step in range(1, count):
        pairs = [(j, (j + direction * step) % count) for j in range(count)]
        moved.append(lax.ppermute(blocks[step], axis, pairs))
    return moved


def per_device(
    spectra,
    psf_blocks,
    observed,
    bad_mask,
    trace_tile,
    trace_slot,
    trace_source,
    trace_block,
    psf_index,
):
    tile_count = lax.axis_size("tile")
    dither_count = lax.axis_size("dither")
    entry_count = trace_slot.shape[0]
    capacity = 2 * entry_count // tile_count
    table_count, bin_count, pixel_count = psf_blocks.shape
    source_count = spectra.shape[0]
    block_count = spectra.shape[1] // bin_count
    row_count = source_count * block_count
    slot_count = observed.shape[1]
    send_count = tile_count * capacity

    target = trace_tile[:, 0]
    kinds = psf_index
    spec_rows = trace_source[:, 0] * block_count + trace_block
    member = one_hot_rows(target, tile_count)
    entry_ids = jnp.arange(entry_count, dtype=jnp.int32)
    up_to = (entry_ids[None, :] <= entry_ids[:, None]).astype(jnp.bfloat16)
    running = select_dot(up_to, member)
    position = jnp.sum((running - 1.0) * member.astype(jnp.float32), axis=1).astype(jnp.int32)
    shift = (target - lax.axis_index("tile")) % tile_count
    dest = shift * capacity + position

    gather_spec = one_hot_rows(spec_rows, row_count)
    spec_values = select_dot(gather_spec, spectra.reshape(row_count, bin_count)).astype(jnp.bfloat16)
    psf_flat = psf_blocks.reshape(table_count * bin_count, pixel_count)
    traces = select_dot(spread_by_kind(spec_values, kinds, table_count), psf_flat).astype(jnp.bfloat16)
    slot_parts = jnp.stack([trace_slot // 256, trace_slot % 256], axis=1).astype(jnp.bfloat16)
    code_rows = -(-2 * capacity // pixel_count)
    places = [one_hot_rows(dest - step * capacity, capacity) for step in range(tile_count)]
    with_codes = jnp.concatenate([traces, slot_parts], axis=1)
    send = []
    for step in range(tile_count):
        placed = select_dot_t(places[step], with_codes).astype(jnp.bfloat16)
        codes = placed[:, pixel_count:].T.reshape(2 * capacity)
        codes = jnp.pad(codes, (0, code_rows * pixel_count - 2 * capacity))
        send.append(
            jnp.concatenate([placed[:, :pixel_count], codes.reshape(code_rows, pixel_count)], axis=0)
        )
    got = exchange(send, "tile", 1)
    got_traces = [block[:capacity] for block in got]
    got_slots = []
    for block in got:
        codes = block[capacity:].reshape(code_rows * pixel_count)[: 2 * capacity]
        codes = codes.astype(jnp.int32).reshape(2, capacity)
        got_slots.append(codes[0] * 256 + codes[1])

    at_slot = [one_hot_rows(slots, slot_count) for slots in got_slots]
    partial_value = sum(select_dot_t(a, b) for a, b in zip(at_slot, got_traces))
    model_image = swap_add(partial_value, "band")
    residual = (
        bad_mask[0].astype(jnp.float32) * (model_image - observed[0].astype(jnp.float32))
    ).astype(jnp.bfloat16)

    under_rows = [select_dot(a, residual).astype(jnp.bfloat16) for a in at_slot]
    returned = exchange(under_rows, "tile", -1)
    entry_rows = sum(select_dot(p, r) for p, r in zip(places, returned)).astype(jnp.bfloat16)
    back_table = psf_blocks.transpose(0, 2, 1).reshape(table_count * pixel_count, bin_count)
    terms = select_dot(spread_by_kind(entry_rows, kinds, table_count), back_table)
    terms = terms.astype(jnp.bfloat16)

    if dither_count == 2:
        dither = lax.axis_index("dither")
        half_rows = row_count // 2
        own_start = dither * half_rows
        their_rows = one_hot_rows(spec_rows - (half_rows - own_start), half_rows)
        own_rows = one_hot_rows(spec_rows - own_start, half_rows)
        theirs = select_dot_t(their_rows, terms).reshape(source_count // 2, block_count * bin_count)
        sent = lax.ppermute(theirs.astype(jnp.bfloat16), "dither", [(0, 1), (1, 0)])
        mine = select_dot_t(own_rows, terms).reshape(source_count // 2, block_count * bin_count)
        gradient = mine + sent.astype(jnp.float32)
    else:
        local_grad = select_dot_t(gather_spec, terms)
        local_grad = local_grad.reshape(source_count, block_count * bin_count)
        gradient = lax.psum_scatter(local_grad, "dither", scatter_dimension=0, tiled=True)
    return (gradient, residual[None])


def solution(mesh):
    in_specs = (
        P(("groups", "tile"), "band"),
        P(),
        P(("groups", "dither"), "tile", None),
        P(("groups", "dither"), "tile", None),
        P(("groups", "tile", "dither", "band"), None),
        P(("groups", "tile", "dither", "band")),
        P(("groups", "tile", "dither", "band"), None),
        P(("groups", "tile", "dither", "band")),
        P(("groups", "tile", "dither", "band")),
    )
    out_specs = (P(("groups", "tile", "dither"), "band"), P(("groups", "dither"), "tile", None))
    return jax.shard_map(
        per_device, mesh=mesh, in_specs=in_specs, out_specs=out_specs, check_vma=False
    )
```

```python
import functools

import jax
import jax.numpy as jnp
from jax import lax
from jax.sharding import PartitionSpec as P


def one_hot_rows(index, width):
    return (index[:, None] == jnp.arange(width, dtype=jnp.int32)[None, :]).astype(jnp.bfloat16)


def select_dot(selector, values, precision=None):
    return jnp.dot(selector, values, preferred_element_type=jnp.float32, precision=precision)


def select_dot_t(selector, values, precision=None):
    return lax.dot_general(
        selector,
        values,
        (((0,), (0,)), ((), ())),
        preferred_element_type=jnp.float32,
        precision=precision,
    )


def spread_by_kind(values, kinds, table_count):
    chosen = kinds[:, None, None] == jnp.arange(table_count, dtype=jnp.int32)[None, :, None]
    spread = jnp.where(chosen, values[:, None, :], jnp.zeros((), values.dtype))
    return spread.reshape(values.shape[0], table_count * values.shape[1])


def swap_add(value, axis):
    count = lax.axis_size(axis)
    if count == 2:
        return value + lax.ppermute(value, axis, [(0, 1), (1, 0)])
    return lax.psum(value, axis)


def exchange(blocks, axis, direction):
    count = lax.axis_size(axis)
    moved = [blocks[0]]
    for step in range(1, count):
        pairs = [(j, (j + direction * step) % count) for j in range(count)]
        moved.append(lax.ppermute(blocks[step], axis, pairs))
    return moved


def per_device(
    spectra,
    psf_blocks,
    observed,
    bad_mask,
    trace_tile,
    trace_slot,
    trace_source,
    trace_block,
    psf_index,
):
    tile_count = lax.axis_size("tile")
    dither_count = lax.axis_size("dither")
    entry_count = trace_slot.shape[0]
    capacity = 2 * entry_count // tile_count
    table_count, bin_count, pixel_count = psf_blocks.shape
    source_count = spectra.shape[0]
    block_count = spectra.shape[1] // bin_count
    row_count = source_count * block_count
    slot_count = observed.shape[1]
    send_count = tile_count * capacity

    target = trace_tile[:, 0]
    kinds = psf_index
    spec_rows = trace_source[:, 0] * block_count + trace_block
    member = one_hot_rows(target, tile_count)
    entry_ids = jnp.arange(entry_count, dtype=jnp.int32)
    up_to = (entry_ids[None, :] <= entry_ids[:, None]).astype(jnp.bfloat16)
    running = select_dot(up_to, member)
    position = jnp.sum((running - 1.0) * member.astype(jnp.float32), axis=1).astype(jnp.int32)
    shift = (target - lax.axis_index("tile")) % tile_count
    dest = shift * capacity + position

    gather_spec = one_hot_rows(spec_rows, row_count)
    spec_values = select_dot(gather_spec, spectra.reshape(row_count, bin_count)).astype(jnp.bfloat16)
    psf_flat = psf_blocks.reshape(table_count * bin_count, pixel_count)
    traces = select_dot(spread_by_kind(spec_values, kinds, table_count), psf_flat).astype(jnp.bfloat16)
    slot_parts = jnp.stack([trace_slot // 256, trace_slot % 256], axis=1).astype(jnp.bfloat16)
    code_rows = -(-2 * capacity // pixel_count)
    places = [one_hot_rows(dest - step * capacity, capacity) for step in range(tile_count)]
    marked_rows = spec_rows + 1
    local_parts = jnp.stack([marked_rows // 256, marked_rows % 256, kinds], axis=1).astype(jnp.bfloat16)
    with_codes = jnp.concatenate([traces, slot_parts, local_parts], axis=1)
    send = []
    block_rows = []
    block_kinds = []
    for step in range(tile_count):
        placed = select_dot_t(places[step], with_codes)
        codes = placed[:, pixel_count : pixel_count + 2].astype(jnp.bfloat16).T.reshape(2 * capacity)
        codes = jnp.pad(codes, (0, code_rows * pixel_count - 2 * capacity))
        send.append(
            jnp.concatenate(
                [
                    placed[:, :pixel_count].astype(jnp.bfloat16),
                    codes.reshape(code_rows, pixel_count),
                ],
                axis=0,
            )
        )
        local = placed[:, pixel_count + 2 :].astype(jnp.int32)
        block_rows.append(local[:, 0] * 256 + local[:, 1] - 1)
        block_kinds.append(local[:, 2])
    got = exchange(send, "tile", 1)
    got_traces = [block[:capacity] for block in got]
    got_slots = []
    for block in got:
        codes = block[capacity:].reshape(code_rows * pixel_count)[: 2 * capacity]
        codes = codes.astype(jnp.int32).reshape(2, capacity)
        got_slots.append(codes[0] * 256 + codes[1])

    at_slot = [one_hot_rows(slots, slot_count) for slots in got_slots]
    partial_value = sum(select_dot_t(a, b) for a, b in zip(at_slot, got_traces))
    model_image = swap_add(partial_value, "band")
    residual = (
        bad_mask[0].astype(jnp.float32) * (model_image - observed[0].astype(jnp.float32))
    ).astype(jnp.bfloat16)

    under_rows = [select_dot(a, residual).astype(jnp.bfloat16) for a in at_slot]
    returned = exchange(under_rows, "tile", -1)
    back_table = psf_blocks.transpose(0, 2, 1).reshape(table_count * pixel_count, bin_count)
    block_terms = [
        select_dot(spread_by_kind(rows, kinds_here, table_count), back_table).astype(jnp.bfloat16)
        for rows, kinds_here in zip(returned, block_kinds)
    ]

    def gathered(offset, width):
        parts = [
            select_dot_t(one_hot_rows(rows - offset, width), terms)
            for rows, terms in zip(block_rows, block_terms)
        ]
        return functools.reduce(jnp.add, parts)

    if dither_count == 2:
        dither = lax.axis_index("dither")
        half_rows = row_count // 2
        own_start = dither * half_rows
        theirs = gathered(half_rows - own_start, half_rows)
        theirs = theirs.reshape(source_count // 2, block_count * bin_count)
        sent = lax.ppermute(theirs.astype(jnp.bfloat16), "dither", [(0, 1), (1, 0)])
        mine = gathered(own_start, half_rows).reshape(source_count // 2, block_count * bin_count)
        gradient = mine + sent.astype(jnp.float32)
    else:
        local_grad = gathered(0, row_count).reshape(source_count, block_count * bin_count)
        gradient = lax.psum_scatter(local_grad, "dither", scatter_dimension=0, tiled=True)
    return (gradient, residual[None])


def solution(mesh):
    in_specs = (
        P(("groups", "tile"), "band"),
        P(),
        P(("groups", "dither"), "tile", None),
        P(("groups", "dither"), "tile", None),
        P(("groups", "tile", "dither", "band"), None),
        P(("groups", "tile", "dither", "band")),
        P(("groups", "tile", "dither", "band"), None),
        P(("groups", "tile", "dither", "band")),
        P(("groups", "tile", "dither", "band")),
    )
    out_specs = (P(("groups", "tile", "dither"), "band"), P(("groups", "dither"), "tile", None))
    return jax.shard_map(
        per_device, mesh=mesh, in_specs=in_specs, out_specs=out_specs, check_vma=False
    )
```

```python
import jax
import jax.numpy as jnp
from jax import lax
from jax.experimental import pallas as pl
from jax.sharding import PartitionSpec as P


def source_kernel(rows_ref, kinds_ref, dest_ref, slots_ref, spectra_ref, psf_ref, blocks_ref, codes_ref):
    entry_count = rows_ref.shape[0]
    row_count = spectra_ref.shape[0]
    table_count = psf_ref.shape[0]
    tile_count, capacity, pixel_count = blocks_ref.shape
    gather = rows_ref[...] == lax.broadcasted_iota(jnp.int32, (entry_count, row_count), 1)
    spec = jnp.dot(
        gather.astype(jnp.bfloat16), spectra_ref[...], preferred_element_type=jnp.float32
    ).astype(jnp.bfloat16)
    kinds = kinds_ref[...]
    acc = jnp.zeros((entry_count, pixel_count), jnp.float32)
    for kind in range(table_count):
        chosen = jnp.where(kinds == kind, spec, jnp.zeros_like(spec))
        acc = acc + jnp.dot(chosen, psf_ref[kind], preferred_element_type=jnp.float32)
    traces = acc.astype(jnp.bfloat16)
    dest = dest_ref[...]
    slots = slots_ref[...]
    for step in range(tile_count):
        spots = lax.broadcasted_iota(jnp.int32, (capacity, entry_count), 0) + step * capacity
        place = (dest == spots).astype(jnp.bfloat16)
        blocks_ref[step] = jnp.dot(place, traces, preferred_element_type=jnp.float32).astype(
            jnp.bfloat16
        )
        codes_ref[step] = lax.dot_general(
            slots, place, (((1,), (1,)), ((), ())), preferred_element_type=jnp.float32
        )


def source_forward(spec_rows, kinds, dest, trace_slot, spectra_flat, psf_blocks, tile_count, capacity):
    entry_count = spec_rows.shape[0]
    pixel_count = psf_blocks.shape[2]
    slots = jnp.zeros((8, entry_count), jnp.bfloat16)
    slots = slots.at[0].set((trace_slot // 256).astype(jnp.bfloat16))
    slots = slots.at[1].set((trace_slot % 256).astype(jnp.bfloat16))
    return pl.pallas_call(
        source_kernel,
        out_shape=(
            jax.ShapeDtypeStruct((tile_count, capacity, pixel_count), jnp.bfloat16),
            jax.ShapeDtypeStruct((tile_count, 8, capacity), jnp.float32),
        ),
    )(spec_rows[:, None], kinds[:, None], dest[None, :], slots, spectra_flat, psf_blocks)


def one_hot_rows(index, width):
    return (index[:, None] == jnp.arange(width, dtype=jnp.int32)[None, :]).astype(jnp.bfloat16)


def select_dot(selector, values, precision=None):
    return jnp.dot(selector, values, preferred_element_type=jnp.float32, precision=precision)


def select_dot_t(selector, values, precision=None):
    return lax.dot_general(
        selector,
        values,
        (((0,), (0,)), ((), ())),
        preferred_element_type=jnp.float32,
        precision=precision,
    )


def spread_by_kind(values, kinds, table_count):
    chosen = kinds[:, None, None] == jnp.arange(table_count, dtype=jnp.int32)[None, :, None]
    spread = jnp.where(chosen, values[:, None, :], jnp.zeros((), values.dtype))
    return spread.reshape(values.shape[0], table_count * values.shape[1])


def swap_add(value, axis):
    count = lax.axis_size(axis)
    if count == 2:
        return value + lax.ppermute(value, axis, [(0, 1), (1, 0)])
    return lax.psum(value, axis)


def exchange(blocks, axis, direction):
    count = lax.axis_size(axis)
    moved = [blocks[0]]
    for step in range(1, count):
        pairs = [(j, (j + direction * step) % count) for j in range(count)]
        moved.append(lax.ppermute(blocks[step], axis, pairs))
    return moved


def per_device(
    spectra,
    psf_blocks,
    observed,
    bad_mask,
    trace_tile,
    trace_slot,
    trace_source,
    trace_block,
    psf_index,
):
    tile_count = lax.axis_size("tile")
    dither_count = lax.axis_size("dither")
    entry_count = trace_slot.shape[0]
    capacity = 2 * entry_count // tile_count
    table_count, bin_count, pixel_count = psf_blocks.shape
    source_count = spectra.shape[0]
    block_count = spectra.shape[1] // bin_count
    row_count = source_count * block_count
    slot_count = observed.shape[1]
    send_count = tile_count * capacity

    target = trace_tile[:, 0]
    kinds = psf_index
    spec_rows = trace_source[:, 0] * block_count + trace_block
    member = one_hot_rows(target, tile_count)
    entry_ids = jnp.arange(entry_count, dtype=jnp.int32)
    up_to = (entry_ids[None, :] <= entry_ids[:, None]).astype(jnp.bfloat16)
    running = select_dot(up_to, member)
    position = jnp.sum((running - 1.0) * member.astype(jnp.float32), axis=1).astype(jnp.int32)
    shift = (target - lax.axis_index("tile")) % tile_count
    dest = shift * capacity + position

    gather_spec = one_hot_rows(spec_rows, row_count)
    code_rows = -(-2 * capacity // pixel_count)
    placed, placed_codes = source_forward(
        spec_rows,
        kinds,
        dest,
        trace_slot,
        spectra.reshape(row_count, bin_count),
        psf_blocks,
        tile_count,
        capacity,
    )
    codes = placed_codes[:, :2].astype(jnp.bfloat16).reshape(tile_count, 2 * capacity)
    codes = jnp.pad(codes, ((0, 0), (0, code_rows * pixel_count - 2 * capacity)))
    send = jnp.concatenate([placed, codes.reshape(tile_count, code_rows, pixel_count)], axis=1)
    send = [send[step] for step in range(tile_count)]
    places = [one_hot_rows(dest - step * capacity, capacity) for step in range(tile_count)]
    got = exchange(send, "tile", 1)
    got_traces = [block[:capacity] for block in got]
    got_slots = []
    for block in got:
        codes = block[capacity:].reshape(code_rows * pixel_count)[: 2 * capacity]
        codes = codes.astype(jnp.int32).reshape(2, capacity)
        got_slots.append(codes[0] * 256 + codes[1])

    at_slot = [one_hot_rows(slots, slot_count) for slots in got_slots]
    partial_value = sum(select_dot_t(a, b) for a, b in zip(at_slot, got_traces))
    model_image = swap_add(partial_value, "band")
    residual = (
        bad_mask[0].astype(jnp.float32) * (model_image - observed[0].astype(jnp.float32))
    ).astype(jnp.bfloat16)

    under_rows = [select_dot(a, residual).astype(jnp.bfloat16) for a in at_slot]
    returned = exchange(under_rows, "tile", -1)
    entry_rows = sum(select_dot(p, r) for p, r in zip(places, returned)).astype(jnp.bfloat16)
    back_table = psf_blocks.transpose(0, 2, 1).reshape(table_count * pixel_count, bin_count)
    terms = select_dot(spread_by_kind(entry_rows, kinds, table_count), back_table)
    terms = terms.astype(jnp.bfloat16)

    if dither_count == 2:
        dither = lax.axis_index("dither")
        half_rows = row_count // 2
        own_start = dither * half_rows
        their_rows = one_hot_rows(spec_rows - (half_rows - own_start), half_rows)
        own_rows = one_hot_rows(spec_rows - own_start, half_rows)
        theirs = select_dot_t(their_rows, terms).reshape(source_count // 2, block_count * bin_count)
        sent = lax.ppermute(theirs.astype(jnp.bfloat16), "dither", [(0, 1), (1, 0)])
        mine = select_dot_t(own_rows, terms).reshape(source_count // 2, block_count * bin_count)
        gradient = mine + sent.astype(jnp.float32)
    else:
        local_grad = select_dot_t(gather_spec, terms)
        local_grad = local_grad.reshape(source_count, block_count * bin_count)
        gradient = lax.psum_scatter(local_grad, "dither", scatter_dimension=0, tiled=True)
    return (gradient, residual[None])


def solution(mesh):
    in_specs = (
        P(("groups", "tile"), "band"),
        P(),
        P(("groups", "dither"), "tile", None),
        P(("groups", "dither"), "tile", None),
        P(("groups", "tile", "dither", "band"), None),
        P(("groups", "tile", "dither", "band")),
        P(("groups", "tile", "dither", "band"), None),
        P(("groups", "tile", "dither", "band")),
        P(("groups", "tile", "dither", "band")),
    )
    out_specs = (P(("groups", "tile", "dither"), "band"), P(("groups", "dither"), "tile", None))
    return jax.shard_map(
        per_device, mesh=mesh, in_specs=in_specs, out_specs=out_specs, check_vma=False
    )
```

```python
import functools

import jax
import jax.numpy as jnp
from jax import lax
from jax.sharding import PartitionSpec as P


def one_hot_rows(index, width):
    return (index[:, None] == jnp.arange(width, dtype=jnp.int32)[None, :]).astype(jnp.bfloat16)


def select_dot(selector, values, precision=None):
    return jnp.dot(selector, values, preferred_element_type=jnp.float32, precision=precision)


def select_dot_t(selector, values, precision=None):
    return lax.dot_general(
        selector,
        values,
        (((0,), (0,)), ((), ())),
        preferred_element_type=jnp.float32,
        precision=precision,
    )


def spread_by_kind(values, kinds, table_count):
    chosen = kinds[:, None, None] == jnp.arange(table_count, dtype=jnp.int32)[None, :, None]
    spread = jnp.where(chosen, values[:, None, :], jnp.zeros((), values.dtype))
    return spread.reshape(values.shape[0], table_count * values.shape[1])


def swap_add(value, axis):
    count = lax.axis_size(axis)
    if count == 2:
        return value + lax.ppermute(value, axis, [(0, 1), (1, 0)])
    return lax.psum(value, axis)


def exchange(blocks, axis, direction):
    count = lax.axis_size(axis)
    moved = [blocks[0]]
    for step in range(1, count):
        pairs = [(j, (j + direction * step) % count) for j in range(count)]
        moved.append(lax.ppermute(blocks[step], axis, pairs))
    return moved


def per_device(
    spectra,
    psf_blocks,
    observed,
    bad_mask,
    trace_tile,
    trace_slot,
    trace_source,
    trace_block,
    psf_index,
):
    tile_count = lax.axis_size("tile")
    dither_count = lax.axis_size("dither")
    entry_count = trace_slot.shape[0]
    capacity = 2 * entry_count // tile_count
    table_count, bin_count, pixel_count = psf_blocks.shape
    source_count = spectra.shape[0]
    block_count = spectra.shape[1] // bin_count
    row_count = source_count * block_count
    slot_count = observed.shape[1]
    send_count = tile_count * capacity

    target = trace_tile[:, 0]
    kinds = psf_index
    spec_rows = trace_source[:, 0] * block_count + trace_block
    member = one_hot_rows(target, tile_count)
    entry_ids = jnp.arange(entry_count, dtype=jnp.int32)
    up_to = (entry_ids[None, :] <= entry_ids[:, None]).astype(jnp.bfloat16)
    running = select_dot(up_to, member)
    position = jnp.sum((running - 1.0) * member.astype(jnp.float32), axis=1).astype(jnp.int32)
    shift = (target - lax.axis_index("tile")) % tile_count
    dest = shift * capacity + position

    gather_spec = one_hot_rows(spec_rows, row_count)
    spec_values = select_dot(gather_spec, spectra.reshape(row_count, bin_count)).astype(jnp.bfloat16)
    psf_flat = psf_blocks.reshape(table_count * bin_count, pixel_count)
    traces = select_dot(spread_by_kind(spec_values, kinds, table_count), psf_flat).astype(jnp.bfloat16)
    slot_parts = jnp.stack([trace_slot // 256, trace_slot % 256], axis=1).astype(jnp.bfloat16)
    code_rows = -(-2 * capacity // pixel_count)
    places = [one_hot_rows(dest - step * capacity, capacity) for step in range(tile_count)]
    send = []
    for step in range(tile_count):
        codes = select_dot_t(slot_parts, places[step]).astype(jnp.bfloat16).reshape(2 * capacity)
        codes = jnp.pad(codes, (0, code_rows * pixel_count - 2 * capacity))
        block = select_dot_t(places[step], traces).astype(jnp.bfloat16)
        send.append(jnp.concatenate([block, codes.reshape(code_rows, pixel_count)], axis=0))
    got = exchange(send, "tile", 1)
    def decoded(block):
        codes = block[capacity:].reshape(code_rows * pixel_count)[: 2 * capacity]
        codes = codes.astype(jnp.int32).reshape(2, capacity)
        return block[:capacity], codes[0] * 256 + codes[1]

    got_traces, got_slots = zip(*[decoded(block) for block in got])
    at_slot = [one_hot_rows(slots, slot_count) for slots in got_slots]
    if lax.axis_size("band") == 2:
        band = lax.axis_index("band")
        half = slot_count // 2
        low = band * half
        pairs = [(0, 1), (1, 0)]
        partner = [decoded(lax.ppermute(block, "band", pairs)) for block in got]
        parts = [
            select_dot_t(one_hot_rows(slots - low, half), traces)
            for traces, slots in list(zip(got_traces, got_slots)) + partner
        ]
        model_half = functools.reduce(jnp.add, parts)
        observed_half = lax.dynamic_slice_in_dim(observed[0], low, half, axis=0)
        mask_half = lax.dynamic_slice_in_dim(bad_mask[0], low, half, axis=0)
        residual_half = (
            mask_half.astype(jnp.float32) * (model_half - observed_half.astype(jnp.float32))
        ).astype(jnp.bfloat16)
        other_half = lax.ppermute(residual_half, "band", pairs)
        residual = jnp.concatenate(
            [
                jnp.where(band == 0, residual_half, other_half),
                jnp.where(band == 0, other_half, residual_half),
            ],
            axis=0,
        )
    else:
        partial_value = functools.reduce(
            jnp.add, [select_dot_t(a, b) for a, b in zip(at_slot, got_traces)]
        )
        model_image = lax.psum(partial_value, "band")
        residual = (
            bad_mask[0].astype(jnp.float32) * (model_image - observed[0].astype(jnp.float32))
        ).astype(jnp.bfloat16)

    under_rows = [select_dot(a, residual).astype(jnp.bfloat16) for a in at_slot]
    returned = exchange(under_rows, "tile", -1)
    entry_rows = sum(select_dot(p, r) for p, r in zip(places, returned)).astype(jnp.bfloat16)
    back_table = psf_blocks.transpose(0, 2, 1).reshape(table_count * pixel_count, bin_count)
    terms = select_dot(spread_by_kind(entry_rows, kinds, table_count), back_table)
    terms = terms.astype(jnp.bfloat16)

    if dither_count == 2:
        dither = lax.axis_index("dither")
        half_rows = row_count // 2
        own_start = dither * half_rows
        their_rows = one_hot_rows(spec_rows - (half_rows - own_start), half_rows)
        own_rows = one_hot_rows(spec_rows - own_start, half_rows)
        theirs = select_dot_t(their_rows, terms).reshape(source_count // 2, block_count * bin_count)
        sent = lax.ppermute(theirs.astype(jnp.bfloat16), "dither", [(0, 1), (1, 0)])
        mine = select_dot_t(own_rows, terms).reshape(source_count // 2, block_count * bin_count)
        gradient = mine + sent.astype(jnp.float32)
    else:
        local_grad = select_dot_t(gather_spec, terms)
        local_grad = local_grad.reshape(source_count, block_count * bin_count)
        gradient = lax.psum_scatter(local_grad, "dither", scatter_dimension=0, tiled=True)
    return (gradient, residual[None])


def solution(mesh):
    in_specs = (
        P(("groups", "tile"), "band"),
        P(),
        P(("groups", "dither"), "tile", None),
        P(("groups", "dither"), "tile", None),
        P(("groups", "tile", "dither", "band"), None),
        P(("groups", "tile", "dither", "band")),
        P(("groups", "tile", "dither", "band"), None),
        P(("groups", "tile", "dither", "band")),
        P(("groups", "tile", "dither", "band")),
    )
    out_specs = (P(("groups", "tile", "dither"), "band"), P(("groups", "dither"), "tile", None))
    return jax.shard_map(
        per_device, mesh=mesh, in_specs=in_specs, out_specs=out_specs, check_vma=False
    )
```

```python
import jax
import jax.numpy as jnp
from jax import lax
from jax.sharding import PartitionSpec as P


def one_hot_rows(index, width):
    return (index[:, None] == jnp.arange(width, dtype=jnp.int32)[None, :]).astype(jnp.bfloat16)


def select_dot(selector, values, precision=None):
    return jnp.dot(selector, values, preferred_element_type=jnp.float32, precision=precision)


def select_dot_t(selector, values, precision=None):
    return lax.dot_general(
        selector,
        values,
        (((0,), (0,)), ((), ())),
        preferred_element_type=jnp.float32,
        precision=precision,
    )


def spread_by_kind(values, kinds, table_count):
    chosen = kinds[:, None, None] == jnp.arange(table_count, dtype=jnp.int32)[None, :, None]
    spread = jnp.where(chosen, values[:, None, :], jnp.zeros((), values.dtype))
    return spread.reshape(values.shape[0], table_count * values.shape[1])


def swap_add(value, axis):
    count = lax.axis_size(axis)
    if count == 2:
        return value + lax.ppermute(value, axis, [(0, 1), (1, 0)])
    return lax.psum(value, axis)


def exchange(blocks, axis, direction):
    count = lax.axis_size(axis)
    moved = [blocks[0]]
    for step in range(1, count):
        pairs = [(j, (j + direction * step) % count) for j in range(count)]
        moved.append(lax.ppermute(blocks[step], axis, pairs))
    return moved


def per_device(
    spectra,
    psf_blocks,
    observed,
    bad_mask,
    trace_tile,
    trace_slot,
    trace_source,
    trace_block,
    psf_index,
):
    tile_count = lax.axis_size("tile")
    dither_count = lax.axis_size("dither")
    entry_count = trace_slot.shape[0]
    capacity = 2 * entry_count // tile_count
    table_count, bin_count, pixel_count = psf_blocks.shape
    source_count = spectra.shape[0]
    block_count = spectra.shape[1] // bin_count
    row_count = source_count * block_count
    slot_count = observed.shape[1]
    send_count = tile_count * capacity

    target = trace_tile[:, 0]
    kinds = psf_index
    spec_rows = trace_source[:, 0] * block_count + trace_block
    member = one_hot_rows(target, tile_count)
    entry_ids = jnp.arange(entry_count, dtype=jnp.int32)
    up_to = (entry_ids[None, :] <= entry_ids[:, None]).astype(jnp.bfloat16)
    running = select_dot(up_to, member)
    position = jnp.sum((running - 1.0) * member.astype(jnp.float32), axis=1).astype(jnp.int32)
    shift = (target - lax.axis_index("tile")) % tile_count
    dest = shift * capacity + position

    gather_spec = one_hot_rows(spec_rows, row_count)
    spec_values = select_dot(gather_spec, spectra.reshape(row_count, bin_count)).astype(jnp.bfloat16)
    psf_flat = psf_blocks.reshape(table_count * bin_count, pixel_count)
    traces = select_dot(spread_by_kind(spec_values, kinds, table_count), psf_flat).astype(jnp.bfloat16)
    slot_parts = jnp.stack([trace_slot // 256, trace_slot % 256], axis=1).astype(jnp.bfloat16)
    code_rows = -(-2 * capacity // pixel_count)
    places = [one_hot_rows(dest - step * capacity, capacity) for step in range(tile_count)]
    send = []
    for step in range(tile_count):
        codes = select_dot_t(slot_parts, places[step]).astype(jnp.bfloat16).reshape(2 * capacity)
        codes = jnp.pad(codes, (0, code_rows * pixel_count - 2 * capacity))
        block = select_dot_t(places[step], traces).astype(jnp.bfloat16)
        send.append(jnp.concatenate([block, codes.reshape(code_rows, pixel_count)], axis=0))
    got = exchange(send, "tile", 1)
    got_traces = [block[:capacity] for block in got]
    got_slots = []
    for block in got:
        codes = block[capacity:].reshape(code_rows * pixel_count)[: 2 * capacity]
        codes = codes.astype(jnp.int32).reshape(2, capacity)
        got_slots.append(codes[0] * 256 + codes[1])

    local_slot = one_hot_rows(got_slots[0], slot_count)
    remote_slot = one_hot_rows(jnp.concatenate(got_slots[1:]), slot_count)
    partial_value = select_dot_t(local_slot, got_traces[0]) + select_dot_t(
        remote_slot, jnp.concatenate(got_traces[1:], axis=0)
    )
    model_image = swap_add(partial_value, "band")
    residual = (
        bad_mask[0].astype(jnp.float32) * (model_image - observed[0].astype(jnp.float32))
    ).astype(jnp.bfloat16)

    remote_rows = select_dot(remote_slot, residual).astype(jnp.bfloat16)
    under_rows = [select_dot(local_slot, residual).astype(jnp.bfloat16)] + [
        remote_rows[step * capacity : (step + 1) * capacity] for step in range(tile_count - 1)
    ]
    returned = exchange(under_rows, "tile", -1)
    entry_rows = sum(select_dot(p, r) for p, r in zip(places, returned)).astype(jnp.bfloat16)
    back_table = psf_blocks.transpose(0, 2, 1).reshape(table_count * pixel_count, bin_count)
    terms = select_dot(spread_by_kind(entry_rows, kinds, table_count), back_table)
    terms = terms.astype(jnp.bfloat16)

    if dither_count == 2:
        dither = lax.axis_index("dither")
        half_rows = row_count // 2
        own_start = dither * half_rows
        their_rows = one_hot_rows(spec_rows - (half_rows - own_start), half_rows)
        own_rows = one_hot_rows(spec_rows - own_start, half_rows)
        theirs = select_dot_t(their_rows, terms).reshape(source_count // 2, block_count * bin_count)
        sent = lax.ppermute(theirs.astype(jnp.bfloat16), "dither", [(0, 1), (1, 0)])
        mine = select_dot_t(own_rows, terms).reshape(source_count // 2, block_count * bin_count)
        gradient = mine + sent.astype(jnp.float32)
    else:
        local_grad = select_dot_t(gather_spec, terms)
        local_grad = local_grad.reshape(source_count, block_count * bin_count)
        gradient = lax.psum_scatter(local_grad, "dither", scatter_dimension=0, tiled=True)
    return (gradient, residual[None])


def solution(mesh):
    in_specs = (
        P(("groups", "tile"), "band"),
        P(),
        P(("groups", "dither"), "tile", None),
        P(("groups", "dither"), "tile", None),
        P(("groups", "tile", "dither", "band"), None),
        P(("groups", "tile", "dither", "band")),
        P(("groups", "tile", "dither", "band"), None),
        P(("groups", "tile", "dither", "band")),
        P(("groups", "tile", "dither", "band")),
    )
    out_specs = (P(("groups", "tile", "dither"), "band"), P(("groups", "dither"), "tile", None))
    return jax.shard_map(
        per_device, mesh=mesh, in_specs=in_specs, out_specs=out_specs, check_vma=False
    )
```

```python
import jax
import jax.numpy as jnp
from jax import lax
from jax.sharding import PartitionSpec as P


def one_hot_rows(index, width):
    return (index[:, None] == jnp.arange(width, dtype=jnp.int32)[None, :]).astype(jnp.bfloat16)


def select_dot(selector, values, precision=None):
    return jnp.dot(selector, values, preferred_element_type=jnp.float32, precision=precision)


def select_dot_t(selector, values, precision=None):
    return lax.dot_general(
        selector,
        values,
        (((0,), (0,)), ((), ())),
        preferred_element_type=jnp.float32,
        precision=precision,
    )


def spread_by_kind(values, kinds, table_count):
    chosen = kinds[:, None, None] == jnp.arange(table_count, dtype=jnp.int32)[None, :, None]
    spread = jnp.where(chosen, values[:, None, :], jnp.zeros((), values.dtype))
    return spread.reshape(values.shape[0], table_count * values.shape[1])


def swap_add(value, axis):
    count = lax.axis_size(axis)
    if count == 2:
        return value + lax.ppermute(value, axis, [(0, 1), (1, 0)])
    return lax.psum(value, axis)


def exchange(blocks, axis, direction):
    count = lax.axis_size(axis)
    moved = [blocks[0]]
    for step in range(1, count):
        pairs = [(j, (j + direction * step) % count) for j in range(count)]
        moved.append(lax.ppermute(blocks[step], axis, pairs))
    return moved


def per_device(
    spectra,
    psf_blocks,
    observed,
    bad_mask,
    trace_tile,
    trace_slot,
    trace_source,
    trace_block,
    psf_index,
):
    tile_count = lax.axis_size("tile")
    dither_count = lax.axis_size("dither")
    entry_count = trace_slot.shape[0]
    capacity = 2 * entry_count // tile_count
    table_count, bin_count, pixel_count = psf_blocks.shape
    source_count = spectra.shape[0]
    block_count = spectra.shape[1] // bin_count
    row_count = source_count * block_count
    slot_count = observed.shape[1]
    send_count = tile_count * capacity

    target = trace_tile[:, 0]
    kinds = psf_index
    spec_rows = trace_source[:, 0] * block_count + trace_block
    member = one_hot_rows(target, tile_count)
    entry_ids = jnp.arange(entry_count, dtype=jnp.int32)
    up_to = (entry_ids[None, :] <= entry_ids[:, None]).astype(jnp.bfloat16)
    running = select_dot(up_to, member)
    position = jnp.sum((running - 1.0) * member.astype(jnp.float32), axis=1).astype(jnp.int32)
    shift = (target - lax.axis_index("tile")) % tile_count
    dest = shift * capacity + position

    gather_spec = one_hot_rows(spec_rows, row_count)
    spec_values = select_dot(gather_spec, spectra.reshape(row_count, bin_count)).astype(jnp.bfloat16)
    psf_flat = psf_blocks.reshape(table_count * bin_count, pixel_count)
    traces = select_dot(spread_by_kind(spec_values, kinds, table_count), psf_flat).astype(jnp.bfloat16)
    slot_parts = jnp.stack([trace_slot // 256, trace_slot % 256], axis=1).astype(jnp.bfloat16)
    code_rows = -(-2 * capacity // pixel_count)
    places = [one_hot_rows(dest - step * capacity, capacity) for step in range(tile_count)]
    with_codes = jnp.concatenate([traces, slot_parts], axis=1)
    send = []
    for step in range(tile_count):
        placed = select_dot_t(places[step], with_codes).astype(jnp.bfloat16)
        codes = placed[:, pixel_count:].T.reshape(2 * capacity)
        codes = jnp.pad(codes, (0, code_rows * pixel_count - 2 * capacity))
        send.append(
            jnp.concatenate([placed[:, :pixel_count], codes.reshape(code_rows, pixel_count)], axis=0)
        )
    got = exchange(send, "tile", 1)
    got_traces = [block[:capacity] for block in got]
    got_slots = []
    for block in got:
        codes = block[capacity:].reshape(code_rows * pixel_count)[: 2 * capacity]
        codes = codes.astype(jnp.int32).reshape(2, capacity)
        got_slots.append(codes[0] * 256 + codes[1])

    local_slot = one_hot_rows(got_slots[0], slot_count)
    remote_slot = one_hot_rows(jnp.concatenate(got_slots[1:]), slot_count)
    partial_value = select_dot_t(local_slot, got_traces[0]) + select_dot_t(
        remote_slot, jnp.concatenate(got_traces[1:], axis=0)
    )
    model_image = swap_add(partial_value, "band")
    residual = (
        bad_mask[0].astype(jnp.float32) * (model_image - observed[0].astype(jnp.float32))
    ).astype(jnp.bfloat16)

    remote_rows = select_dot(remote_slot, residual).astype(jnp.bfloat16)
    under_rows = [select_dot(local_slot, residual).astype(jnp.bfloat16)] + [
        remote_rows[step * capacity : (step + 1) * capacity] for step in range(tile_count - 1)
    ]
    returned = exchange(under_rows, "tile", -1)
    entry_rows = sum(select_dot(p, r) for p, r in zip(places, returned)).astype(jnp.bfloat16)
    back_table = psf_blocks.transpose(0, 2, 1).reshape(table_count * pixel_count, bin_count)
    terms = select_dot(spread_by_kind(entry_rows, kinds, table_count), back_table)
    terms = terms.astype(jnp.bfloat16)

    if dither_count == 2:
        dither = lax.axis_index("dither")
        local_grad = select_dot_t(gather_spec, terms).reshape(2, row_count // 2, bin_count)
        halves = local_grad.reshape(2, source_count // 2, block_count * bin_count)
        theirs = jnp.where(dither == 0, halves[1], halves[0])
        mine = jnp.where(dither == 0, halves[0], halves[1])
        sent = lax.ppermute(theirs.astype(jnp.bfloat16), "dither", [(0, 1), (1, 0)])
        gradient = mine + sent.astype(jnp.float32)
    else:
        local_grad = select_dot_t(gather_spec, terms)
        local_grad = local_grad.reshape(source_count, block_count * bin_count)
        gradient = lax.psum_scatter(local_grad, "dither", scatter_dimension=0, tiled=True)
    return (gradient, residual[None])


def solution(mesh):
    in_specs = (
        P(("groups", "tile"), "band"),
        P(),
        P(("groups", "dither"), "tile", None),
        P(("groups", "dither"), "tile", None),
        P(("groups", "tile", "dither", "band"), None),
        P(("groups", "tile", "dither", "band")),
        P(("groups", "tile", "dither", "band"), None),
        P(("groups", "tile", "dither", "band")),
        P(("groups", "tile", "dither", "band")),
    )
    out_specs = (P(("groups", "tile", "dither"), "band"), P(("groups", "dither"), "tile", None))
    return jax.shard_map(
        per_device, mesh=mesh, in_specs=in_specs, out_specs=out_specs, check_vma=False
    )
```

```python
import jax
import jax.numpy as jnp
from jax import lax
from jax.sharding import PartitionSpec as P


def one_hot_rows(index, width):
    return (index[:, None] == jnp.arange(width, dtype=jnp.int32)[None, :]).astype(jnp.bfloat16)


def select_dot(selector, values, precision=None):
    return jnp.dot(selector, values, preferred_element_type=jnp.float32, precision=precision)


def select_dot_t(selector, values, precision=None):
    return lax.dot_general(
        selector,
        values,
        (((0,), (0,)), ((), ())),
        preferred_element_type=jnp.float32,
        precision=precision,
    )


def spread_by_kind(values, kinds, table_count):
    chosen = kinds[:, None, None] == jnp.arange(table_count, dtype=jnp.int32)[None, :, None]
    spread = jnp.where(chosen, values[:, None, :], jnp.zeros((), values.dtype))
    return spread.reshape(values.shape[0], table_count * values.shape[1])


def swap_add(value, axis):
    count = lax.axis_size(axis)
    if count == 2:
        return value + lax.ppermute(value, axis, [(0, 1), (1, 0)])
    return lax.psum(value, axis)


def exchange(blocks, axis, direction):
    count = lax.axis_size(axis)
    moved = [blocks[0]]
    for step in range(1, count):
        pairs = [(j, (j + direction * step) % count) for j in range(count)]
        moved.append(lax.ppermute(blocks[step], axis, pairs))
    return moved


def per_device(
    spectra,
    psf_blocks,
    observed,
    bad_mask,
    trace_tile,
    trace_slot,
    trace_source,
    trace_block,
    psf_index,
):
    tile_count = lax.axis_size("tile")
    dither_count = lax.axis_size("dither")
    entry_count = trace_slot.shape[0]
    capacity = 2 * entry_count // tile_count
    table_count, bin_count, pixel_count = psf_blocks.shape
    source_count = spectra.shape[0]
    block_count = spectra.shape[1] // bin_count
    row_count = source_count * block_count
    slot_count = observed.shape[1]
    send_count = tile_count * capacity

    target = trace_tile[:, 0]
    kinds = psf_index
    spec_rows = trace_source[:, 0] * block_count + trace_block
    member = one_hot_rows(target, tile_count)
    entry_ids = jnp.arange(entry_count, dtype=jnp.int32)
    up_to = (entry_ids[None, :] <= entry_ids[:, None]).astype(jnp.bfloat16)
    running = select_dot(up_to, member)
    position = jnp.sum((running - 1.0) * member.astype(jnp.float32), axis=1).astype(jnp.int32)
    shift = (target - lax.axis_index("tile")) % tile_count
    dest = shift * capacity + position

    gather_spec = one_hot_rows(spec_rows, row_count)
    spec_values = select_dot(gather_spec, spectra.reshape(row_count, bin_count)).astype(jnp.bfloat16)
    psf_flat = psf_blocks.reshape(table_count * bin_count, pixel_count)
    traces = select_dot(spread_by_kind(spec_values, kinds, table_count), psf_flat).astype(jnp.bfloat16)
    slot_parts = jnp.stack([trace_slot // 256, trace_slot % 256], axis=1).astype(jnp.bfloat16)
    code_rows = -(-2 * capacity // pixel_count)
    places = [one_hot_rows(dest - step * capacity, capacity) for step in range(tile_count)]
    early = tile_count // 2
    early_parts = jnp.concatenate([slot_parts, kinds[:, None].astype(jnp.bfloat16)], axis=1)
    early_rows = -(-3 * capacity // pixel_count)
    send = []
    for step in range(tile_count):
        if step == early and step > 0:
            values, parts, rows = spec_values, early_parts, early_rows
        else:
            values, parts, rows = traces, slot_parts, code_rows
        width = parts.shape[1]
        codes = select_dot_t(parts, places[step]).astype(jnp.bfloat16).reshape(width * capacity)
        codes = jnp.pad(codes, (0, rows * pixel_count - width * capacity))
        block = select_dot_t(places[step], values).astype(jnp.bfloat16)
        send.append(jnp.concatenate([block, codes.reshape(rows, pixel_count)], axis=0))
    got = exchange(send, "tile", 1)
    got_traces = []
    got_slots = []
    for step, block in enumerate(got):
        width = 3 if step == early and step > 0 else 2
        codes = block[capacity:].reshape(-1)[: width * capacity]
        codes = codes.astype(jnp.int32).reshape(width, capacity)
        got_slots.append(codes[0] * 256 + codes[1])
        if width == 3:
            spread = spread_by_kind(block[:capacity], codes[2], table_count)
            got_traces.append(select_dot(spread, psf_flat).astype(jnp.bfloat16))
        else:
            got_traces.append(block[:capacity])

    at_slot = [one_hot_rows(slots, slot_count) for slots in got_slots]
    partial_value = sum(select_dot_t(a, b) for a, b in zip(at_slot, got_traces))
    model_image = swap_add(partial_value, "band")
    residual = (
        bad_mask[0].astype(jnp.float32) * (model_image - observed[0].astype(jnp.float32))
    ).astype(jnp.bfloat16)

    under_rows = [select_dot(a, residual).astype(jnp.bfloat16) for a in at_slot]
    returned = exchange(under_rows, "tile", -1)
    entry_rows = sum(select_dot(p, r) for p, r in zip(places, returned)).astype(jnp.bfloat16)
    back_table = psf_blocks.transpose(0, 2, 1).reshape(table_count * pixel_count, bin_count)
    terms = select_dot(spread_by_kind(entry_rows, kinds, table_count), back_table)
    terms = terms.astype(jnp.bfloat16)

    if dither_count == 2:
        dither = lax.axis_index("dither")
        half_rows = row_count // 2
        own_start = dither * half_rows
        their_rows = one_hot_rows(spec_rows - (half_rows - own_start), half_rows)
        own_rows = one_hot_rows(spec_rows - own_start, half_rows)
        theirs = select_dot_t(their_rows, terms).reshape(source_count // 2, block_count * bin_count)
        sent = lax.ppermute(theirs.astype(jnp.bfloat16), "dither", [(0, 1), (1, 0)])
        mine = select_dot_t(own_rows, terms).reshape(source_count // 2, block_count * bin_count)
        gradient = mine + sent.astype(jnp.float32)
    else:
        local_grad = select_dot_t(gather_spec, terms)
        local_grad = local_grad.reshape(source_count, block_count * bin_count)
        gradient = lax.psum_scatter(local_grad, "dither", scatter_dimension=0, tiled=True)
    return (gradient, residual[None])


def solution(mesh):
    in_specs = (
        P(("groups", "tile"), "band"),
        P(),
        P(("groups", "dither"), "tile", None),
        P(("groups", "dither"), "tile", None),
        P(("groups", "tile", "dither", "band"), None),
        P(("groups", "tile", "dither", "band")),
        P(("groups", "tile", "dither", "band"), None),
        P(("groups", "tile", "dither", "band")),
        P(("groups", "tile", "dither", "band")),
    )
    out_specs = (P(("groups", "tile", "dither"), "band"), P(("groups", "dither"), "tile", None))
    return jax.shard_map(
        per_device, mesh=mesh, in_specs=in_specs, out_specs=out_specs, check_vma=False
    )
```

```python
import jax
import jax.numpy as jnp
from jax import lax
from jax.sharding import PartitionSpec as P


def one_hot_rows(index, width):
    return (index[:, None] == jnp.arange(width, dtype=jnp.int32)[None, :]).astype(jnp.bfloat16)


def select_dot(selector, values, precision=None):
    return jnp.dot(selector, values, preferred_element_type=jnp.float32, precision=precision)


def select_dot_t(selector, values, precision=None):
    return lax.dot_general(
        selector,
        values,
        (((0,), (0,)), ((), ())),
        preferred_element_type=jnp.float32,
        precision=precision,
    )


def spread_by_kind(values, kinds, table_count):
    chosen = kinds[:, None, None] == jnp.arange(table_count, dtype=jnp.int32)[None, :, None]
    spread = jnp.where(chosen, values[:, None, :], jnp.zeros((), values.dtype))
    return spread.reshape(values.shape[0], table_count * values.shape[1])


def swap_add(value, axis):
    count = lax.axis_size(axis)
    if count == 2:
        return value + lax.ppermute(value, axis, [(0, 1), (1, 0)])
    return lax.psum(value, axis)


def exchange(blocks, axis, direction):
    count = lax.axis_size(axis)
    moved = [blocks[0]]
    for step in range(1, count):
        pairs = [(j, (j + direction * step) % count) for j in range(count)]
        moved.append(lax.ppermute(blocks[step], axis, pairs))
    return moved


def per_device(
    spectra,
    psf_blocks,
    observed,
    bad_mask,
    trace_tile,
    trace_slot,
    trace_source,
    trace_block,
    psf_index,
):
    tile_count = lax.axis_size("tile")
    dither_count = lax.axis_size("dither")
    entry_count = trace_slot.shape[0]
    capacity = 2 * entry_count // tile_count
    table_count, bin_count, pixel_count = psf_blocks.shape
    source_count = spectra.shape[0]
    block_count = spectra.shape[1] // bin_count
    row_count = source_count * block_count
    slot_count = observed.shape[1]
    send_count = tile_count * capacity

    target = trace_tile[:, 0]
    kinds = psf_index
    spec_rows = trace_source[:, 0] * block_count + trace_block
    member = one_hot_rows(target, tile_count)
    entry_ids = jnp.arange(entry_count, dtype=jnp.int32)
    up_to = (entry_ids[None, :] <= entry_ids[:, None]).astype(jnp.bfloat16)
    running = select_dot(up_to, member)
    position = jnp.sum((running - 1.0) * member.astype(jnp.float32), axis=1).astype(jnp.int32)
    shift = (target - lax.axis_index("tile")) % tile_count
    dest = shift * capacity + position

    gather_spec = one_hot_rows(spec_rows, row_count)
    spec_values = select_dot(gather_spec, spectra.reshape(row_count, bin_count)).astype(jnp.bfloat16)
    psf_flat = psf_blocks.reshape(table_count * bin_count, pixel_count)
    traces = select_dot(spread_by_kind(spec_values, kinds, table_count), psf_flat).astype(jnp.bfloat16)
    slot_parts = jnp.stack([trace_slot // 256, trace_slot % 256], axis=1).astype(jnp.bfloat16)
    code_rows = -(-2 * capacity // pixel_count)
    places = [one_hot_rows(dest - step * capacity, capacity) for step in range(tile_count)]
    all_codes = select_dot_t(slot_parts, one_hot_rows(dest, send_count)).astype(jnp.bfloat16)
    all_codes = all_codes.reshape(2, tile_count, capacity)
    send = []
    for step in range(tile_count):
        codes = all_codes[:, step].reshape(2 * capacity)
        codes = jnp.pad(codes, (0, code_rows * pixel_count - 2 * capacity))
        block = select_dot_t(places[step], traces).astype(jnp.bfloat16)
        send.append(jnp.concatenate([block, codes.reshape(code_rows, pixel_count)], axis=0))
    got = exchange(send, "tile", 1)
    got_traces = [block[:capacity] for block in got]
    got_slots = []
    for block in got:
        codes = block[capacity:].reshape(code_rows * pixel_count)[: 2 * capacity]
        codes = codes.astype(jnp.int32).reshape(2, capacity)
        got_slots.append(codes[0] * 256 + codes[1])

    at_slot = [one_hot_rows(slots, slot_count) for slots in got_slots]
    partial_value = sum(select_dot_t(a, b) for a, b in zip(at_slot, got_traces))
    model_image = swap_add(partial_value, "band")
    residual = (
        bad_mask[0].astype(jnp.float32) * (model_image - observed[0].astype(jnp.float32))
    ).astype(jnp.bfloat16)

    under_rows = [select_dot(a, residual).astype(jnp.bfloat16) for a in at_slot]
    returned = exchange(under_rows, "tile", -1)
    entry_rows = sum(select_dot(p, r) for p, r in zip(places, returned)).astype(jnp.bfloat16)
    back_table = psf_blocks.transpose(0, 2, 1).reshape(table_count * pixel_count, bin_count)
    terms = select_dot(spread_by_kind(entry_rows, kinds, table_count), back_table)
    terms = terms.astype(jnp.bfloat16)

    if dither_count == 2:
        dither = lax.axis_index("dither")
        half_rows = row_count // 2
        own_start = dither * half_rows
        their_rows = one_hot_rows(spec_rows - (half_rows - own_start), half_rows)
        own_rows = one_hot_rows(spec_rows - own_start, half_rows)
        theirs = select_dot_t(their_rows, terms).reshape(source_count // 2, block_count * bin_count)
        sent = lax.ppermute(theirs.astype(jnp.bfloat16), "dither", [(0, 1), (1, 0)])
        mine = select_dot_t(own_rows, terms).reshape(source_count // 2, block_count * bin_count)
        gradient = mine + sent.astype(jnp.float32)
    else:
        local_grad = select_dot_t(gather_spec, terms)
        local_grad = local_grad.reshape(source_count, block_count * bin_count)
        gradient = lax.psum_scatter(local_grad, "dither", scatter_dimension=0, tiled=True)
    return (gradient, residual[None])


def solution(mesh):
    in_specs = (
        P(("groups", "tile"), "band"),
        P(),
        P(("groups", "dither"), "tile", None),
        P(("groups", "dither"), "tile", None),
        P(("groups", "tile", "dither", "band"), None),
        P(("groups", "tile", "dither", "band")),
        P(("groups", "tile", "dither", "band"), None),
        P(("groups", "tile", "dither", "band")),
        P(("groups", "tile", "dither", "band")),
    )
    out_specs = (P(("groups", "tile", "dither"), "band"), P(("groups", "dither"), "tile", None))
    return jax.shard_map(
        per_device, mesh=mesh, in_specs=in_specs, out_specs=out_specs, check_vma=False
    )
```

```python
import jax
import jax.numpy as jnp
from jax import lax
from jax.sharding import PartitionSpec as P


def one_hot_rows(index, width):
    return (index[:, None] == jnp.arange(width, dtype=jnp.int32)[None, :]).astype(jnp.bfloat16)


def row_hot(source, block, block_count, start, width):
    rows = start + jnp.arange(width, dtype=jnp.int32)[None, :]
    return (
        (rows // block_count == source[:, None]) & (rows % block_count == block[:, None])
    ).astype(jnp.bfloat16)


def select_dot(selector, values, precision=None):
    return jnp.dot(selector, values, preferred_element_type=jnp.float32, precision=precision)


def select_dot_t(selector, values, precision=None):
    return lax.dot_general(
        selector,
        values,
        (((0,), (0,)), ((), ())),
        preferred_element_type=jnp.float32,
        precision=precision,
    )


def spread_by_kind(values, kinds, table_count):
    chosen = kinds[:, None, None] == jnp.arange(table_count, dtype=jnp.int32)[None, :, None]
    spread = jnp.where(chosen, values[:, None, :], jnp.zeros((), values.dtype))
    return spread.reshape(values.shape[0], table_count * values.shape[1])


def swap_add(value, axis):
    count = lax.axis_size(axis)
    if count == 2:
        return value + lax.ppermute(value, axis, [(0, 1), (1, 0)])
    return lax.psum(value, axis)


def exchange(blocks, axis, direction):
    count = lax.axis_size(axis)
    moved = [blocks[0]]
    for step in range(1, count):
        pairs = [(j, (j + direction * step) % count) for j in range(count)]
        moved.append(lax.ppermute(blocks[step], axis, pairs))
    return moved


def per_device(
    spectra,
    psf_blocks,
    observed,
    bad_mask,
    trace_tile,
    trace_slot,
    trace_source,
    trace_block,
    psf_index,
):
    tile_count = lax.axis_size("tile")
    dither_count = lax.axis_size("dither")
    entry_count = trace_slot.shape[0]
    capacity = 2 * entry_count // tile_count
    table_count, bin_count, pixel_count = psf_blocks.shape
    source_count = spectra.shape[0]
    block_count = spectra.shape[1] // bin_count
    row_count = source_count * block_count
    slot_count = observed.shape[1]
    send_count = tile_count * capacity

    target = trace_tile[:, 0]
    kinds = psf_index
    source_here = trace_source[:, 0]
    member = one_hot_rows(target, tile_count)
    entry_ids = jnp.arange(entry_count, dtype=jnp.int32)
    up_to = (entry_ids[None, :] <= entry_ids[:, None]).astype(jnp.bfloat16)
    running = select_dot(up_to, member)
    position = jnp.sum((running - 1.0) * member.astype(jnp.float32), axis=1).astype(jnp.int32)
    shift = (target - lax.axis_index("tile")) % tile_count
    dest = shift * capacity + position

    gather_spec = row_hot(source_here, trace_block, block_count, 0, row_count)
    spec_values = select_dot(gather_spec, spectra.reshape(row_count, bin_count)).astype(jnp.bfloat16)
    psf_flat = psf_blocks.reshape(table_count * bin_count, pixel_count)
    traces = select_dot(spread_by_kind(spec_values, kinds, table_count), psf_flat).astype(jnp.bfloat16)
    slot_parts = jnp.stack([trace_slot // 256, trace_slot % 256], axis=1).astype(jnp.bfloat16)
    code_rows = -(-2 * capacity // pixel_count)
    places = [one_hot_rows(dest - step * capacity, capacity) for step in range(tile_count)]
    send = []
    for step in range(tile_count):
        codes = select_dot_t(slot_parts, places[step]).astype(jnp.bfloat16).reshape(2 * capacity)
        codes = jnp.pad(codes, (0, code_rows * pixel_count - 2 * capacity))
        block = select_dot_t(places[step], traces).astype(jnp.bfloat16)
        send.append(jnp.concatenate([block, codes.reshape(code_rows, pixel_count)], axis=0))
    got = exchange(send, "tile", 1)
    got_traces = [block[:capacity] for block in got]
    got_slots = []
    for block in got:
        codes = block[capacity:].reshape(code_rows * pixel_count)[: 2 * capacity]
        codes = codes.astype(jnp.int32).reshape(2, capacity)
        got_slots.append(codes[0] * 256 + codes[1])

    at_slot = [one_hot_rows(slots, slot_count) for slots in got_slots]
    partial_value = sum(select_dot_t(a, b) for a, b in zip(at_slot, got_traces))
    model_image = swap_add(partial_value, "band")
    residual = (
        bad_mask[0].astype(jnp.float32) * (model_image - observed[0].astype(jnp.float32))
    ).astype(jnp.bfloat16)

    under_rows = [select_dot(a, residual).astype(jnp.bfloat16) for a in at_slot]
    returned = exchange(under_rows, "tile", -1)
    entry_rows = sum(select_dot(p, r) for p, r in zip(places, returned)).astype(jnp.bfloat16)
    back_table = psf_blocks.transpose(0, 2, 1).reshape(table_count * pixel_count, bin_count)
    terms = select_dot(spread_by_kind(entry_rows, kinds, table_count), back_table)
    terms = terms.astype(jnp.bfloat16)

    if dither_count == 2:
        dither = lax.axis_index("dither")
        half_rows = row_count // 2
        own_start = dither * half_rows
        their_rows = row_hot(source_here, trace_block, block_count, half_rows - own_start, half_rows)
        own_rows = row_hot(source_here, trace_block, block_count, own_start, half_rows)
        theirs = select_dot_t(their_rows, terms).reshape(source_count // 2, block_count * bin_count)
        sent = lax.ppermute(theirs.astype(jnp.bfloat16), "dither", [(0, 1), (1, 0)])
        mine = select_dot_t(own_rows, terms).reshape(source_count // 2, block_count * bin_count)
        gradient = mine + sent.astype(jnp.float32)
    else:
        local_grad = select_dot_t(gather_spec, terms)
        local_grad = local_grad.reshape(source_count, block_count * bin_count)
        gradient = lax.psum_scatter(local_grad, "dither", scatter_dimension=0, tiled=True)
    return (gradient, residual[None])


def solution(mesh):
    in_specs = (
        P(("groups", "tile"), "band"),
        P(),
        P(("groups", "dither"), "tile", None),
        P(("groups", "dither"), "tile", None),
        P(("groups", "tile", "dither", "band"), None),
        P(("groups", "tile", "dither", "band")),
        P(("groups", "tile", "dither", "band"), None),
        P(("groups", "tile", "dither", "band")),
        P(("groups", "tile", "dither", "band")),
    )
    out_specs = (P(("groups", "tile", "dither"), "band"), P(("groups", "dither"), "tile", None))
    return jax.shard_map(
        per_device, mesh=mesh, in_specs=in_specs, out_specs=out_specs, check_vma=False
    )
```

```python
import jax
import jax.numpy as jnp
from jax import lax
from jax.sharding import PartitionSpec as P


def one_hot_rows(index, width):
    return (index[:, None] == jnp.arange(width, dtype=jnp.int32)[None, :]).astype(jnp.bfloat16)


def row_hot(source, block, block_count, start, width):
    rows = start + jnp.arange(width, dtype=jnp.int32)[None, :]
    return (
        (rows // block_count == source[:, None]) & (rows % block_count == block[:, None])
    ).astype(jnp.bfloat16)


def select_dot(selector, values, precision=None):
    return jnp.dot(selector, values, preferred_element_type=jnp.float32, precision=precision)


def select_dot_t(selector, values, precision=None):
    return lax.dot_general(
        selector,
        values,
        (((0,), (0,)), ((), ())),
        preferred_element_type=jnp.float32,
        precision=precision,
    )


def spread_by_kind(values, kinds, table_count):
    chosen = kinds[:, None, None] == jnp.arange(table_count, dtype=jnp.int32)[None, :, None]
    spread = jnp.where(chosen, values[:, None, :], jnp.zeros((), values.dtype))
    return spread.reshape(values.shape[0], table_count * values.shape[1])


def swap_add(value, axis):
    count = lax.axis_size(axis)
    if count == 2:
        return value + lax.ppermute(value, axis, [(0, 1), (1, 0)])
    return lax.psum(value, axis)


def exchange(blocks, axis, direction):
    count = lax.axis_size(axis)
    moved = [blocks[0]]
    for step in range(1, count):
        pairs = [(j, (j + direction * step) % count) for j in range(count)]
        moved.append(lax.ppermute(blocks[step], axis, pairs))
    return moved


def per_device(
    spectra,
    psf_blocks,
    observed,
    bad_mask,
    trace_tile,
    trace_slot,
    trace_source,
    trace_block,
    psf_index,
):
    tile_count = lax.axis_size("tile")
    dither_count = lax.axis_size("dither")
    entry_count = trace_slot.shape[0]
    capacity = 2 * entry_count // tile_count
    table_count, bin_count, pixel_count = psf_blocks.shape
    source_count = spectra.shape[0]
    block_count = spectra.shape[1] // bin_count
    row_count = source_count * block_count
    slot_count = observed.shape[1]
    send_count = tile_count * capacity

    target = trace_tile[:, 0]
    kinds = psf_index
    source_here = trace_source[:, 0]
    member = one_hot_rows(target, tile_count)
    entry_ids = jnp.arange(entry_count, dtype=jnp.int32)
    up_to = (entry_ids[None, :] <= entry_ids[:, None]).astype(jnp.bfloat16)
    running = select_dot(up_to, member)
    position = jnp.sum((running - 1.0) * member.astype(jnp.float32), axis=1).astype(jnp.int32)
    shift = (target - lax.axis_index("tile")) % tile_count
    dest = shift * capacity + position

    source_hot = one_hot_rows(source_here, source_count)
    whole_rows = select_dot(source_hot, spectra).astype(jnp.bfloat16)
    chosen_block = trace_block[:, None, None] == jnp.arange(block_count, dtype=jnp.int32)[None, :, None]
    spec_values = jnp.sum(
        jnp.where(chosen_block, whole_rows.reshape(entry_count, block_count, bin_count), 0.0), axis=1
    ).astype(jnp.bfloat16)
    gather_spec = row_hot(source_here, trace_block, block_count, 0, row_count)
    psf_flat = psf_blocks.reshape(table_count * bin_count, pixel_count)
    traces = select_dot(spread_by_kind(spec_values, kinds, table_count), psf_flat).astype(jnp.bfloat16)
    slot_parts = jnp.stack([trace_slot // 256, trace_slot % 256], axis=1).astype(jnp.bfloat16)
    code_rows = -(-2 * capacity // pixel_count)
    places = [one_hot_rows(dest - step * capacity, capacity) for step in range(tile_count)]
    send = []
    for step in range(tile_count):
        codes = select_dot_t(slot_parts, places[step]).astype(jnp.bfloat16).reshape(2 * capacity)
        codes = jnp.pad(codes, (0, code_rows * pixel_count - 2 * capacity))
        block = select_dot_t(places[step], traces).astype(jnp.bfloat16)
        send.append(jnp.concatenate([block, codes.reshape(code_rows, pixel_count)], axis=0))
    got = exchange(send, "tile", 1)
    got_traces = [block[:capacity] for block in got]
    got_slots = []
    for block in got:
        codes = block[capacity:].reshape(code_rows * pixel_count)[: 2 * capacity]
        codes = codes.astype(jnp.int32).reshape(2, capacity)
        got_slots.append(codes[0] * 256 + codes[1])

    at_slot = [one_hot_rows(slots, slot_count) for slots in got_slots]
    partial_value = sum(select_dot_t(a, b) for a, b in zip(at_slot, got_traces))
    model_image = swap_add(partial_value, "band")
    residual = (
        bad_mask[0].astype(jnp.float32) * (model_image - observed[0].astype(jnp.float32))
    ).astype(jnp.bfloat16)

    under_rows = [select_dot(a, residual).astype(jnp.bfloat16) for a in at_slot]
    returned = exchange(under_rows, "tile", -1)
    entry_rows = sum(select_dot(p, r) for p, r in zip(places, returned)).astype(jnp.bfloat16)
    back_table = psf_blocks.transpose(0, 2, 1).reshape(table_count * pixel_count, bin_count)
    terms = select_dot(spread_by_kind(entry_rows, kinds, table_count), back_table)
    terms = terms.astype(jnp.bfloat16)

    if dither_count == 2:
        dither = lax.axis_index("dither")
        half_rows = row_count // 2
        own_start = dither * half_rows
        half_sources = source_count // 2
        own_first = dither * half_sources
        by_block = spread_by_kind(terms, trace_block, block_count)
        their_hot = one_hot_rows(source_here - (half_sources - own_first), half_sources)
        own_hot = one_hot_rows(source_here - own_first, half_sources)
        theirs = select_dot_t(their_hot, by_block)
        sent = lax.ppermute(theirs.astype(jnp.bfloat16), "dither", [(0, 1), (1, 0)])
        mine = select_dot_t(own_hot, by_block)
        gradient = mine + sent.astype(jnp.float32)
    else:
        local_grad = select_dot_t(gather_spec, terms)
        local_grad = local_grad.reshape(source_count, block_count * bin_count)
        gradient = lax.psum_scatter(local_grad, "dither", scatter_dimension=0, tiled=True)
    return (gradient, residual[None])


def solution(mesh):
    in_specs = (
        P(("groups", "tile"), "band"),
        P(),
        P(("groups", "dither"), "tile", None),
        P(("groups", "dither"), "tile", None),
        P(("groups", "tile", "dither", "band"), None),
        P(("groups", "tile", "dither", "band")),
        P(("groups", "tile", "dither", "band"), None),
        P(("groups", "tile", "dither", "band")),
        P(("groups", "tile", "dither", "band")),
    )
    out_specs = (P(("groups", "tile", "dither"), "band"), P(("groups", "dither"), "tile", None))
    return jax.shard_map(
        per_device, mesh=mesh, in_specs=in_specs, out_specs=out_specs, check_vma=False
    )
```

```python
import jax
import jax.numpy as jnp
from jax import lax
from jax.sharding import PartitionSpec as P


def one_hot_rows(index, width):
    return (index[:, None] == jnp.arange(width, dtype=jnp.int32)[None, :]).astype(jnp.bfloat16)


def row_hot(source, block, block_count, start, width):
    rows = start + jnp.arange(width, dtype=jnp.int32)[None, :]
    return (
        (rows // block_count == source[:, None]) & (rows % block_count == block[:, None])
    ).astype(jnp.bfloat16)


def select_dot(selector, values, precision=None):
    return jnp.dot(selector, values, preferred_element_type=jnp.float32, precision=precision)


def select_dot_t(selector, values, precision=None):
    return lax.dot_general(
        selector,
        values,
        (((0,), (0,)), ((), ())),
        preferred_element_type=jnp.float32,
        precision=precision,
    )


def spread_by_kind(values, kinds, table_count):
    chosen = kinds[:, None, None] == jnp.arange(table_count, dtype=jnp.int32)[None, :, None]
    spread = jnp.where(chosen, values[:, None, :], jnp.zeros((), values.dtype))
    return spread.reshape(values.shape[0], table_count * values.shape[1])


def swap_add(value, axis):
    count = lax.axis_size(axis)
    if count == 2:
        return value + lax.ppermute(value, axis, [(0, 1), (1, 0)])
    return lax.psum(value, axis)


def exchange(blocks, axis, direction):
    count = lax.axis_size(axis)
    moved = [blocks[0]]
    for step in range(1, count):
        pairs = [(j, (j + direction * step) % count) for j in range(count)]
        moved.append(lax.ppermute(blocks[step], axis, pairs))
    return moved


def per_device(
    spectra,
    psf_blocks,
    observed,
    bad_mask,
    trace_tile,
    trace_slot,
    trace_source,
    trace_block,
    psf_index,
):
    tile_count = lax.axis_size("tile")
    dither_count = lax.axis_size("dither")
    entry_count = trace_slot.shape[0]
    capacity = 2 * entry_count // tile_count
    table_count, bin_count, pixel_count = psf_blocks.shape
    source_count = spectra.shape[0]
    block_count = spectra.shape[1] // bin_count
    row_count = source_count * block_count
    slot_count = observed.shape[1]
    send_count = tile_count * capacity

    target = trace_tile[:, 0]
    kinds = psf_index
    source_here = trace_source[:, 0]
    member = one_hot_rows(target, tile_count)
    entry_ids = jnp.arange(entry_count, dtype=jnp.int32)
    up_to = (entry_ids[None, :] <= entry_ids[:, None]).astype(jnp.bfloat16)
    running = select_dot(up_to, member)
    position = jnp.sum((running - 1.0) * member.astype(jnp.float32), axis=1).astype(jnp.int32)
    shift = (target - lax.axis_index("tile")) % tile_count
    dest = shift * capacity + position

    source_hot = one_hot_rows(source_here, source_count)
    whole_rows = select_dot(source_hot, spectra).astype(jnp.bfloat16)
    chosen_block = trace_block[:, None, None] == jnp.arange(block_count, dtype=jnp.int32)[None, :, None]
    spec_values = jnp.sum(
        jnp.where(chosen_block, whole_rows.reshape(entry_count, block_count, bin_count), 0.0), axis=1
    ).astype(jnp.bfloat16)
    gather_spec = row_hot(source_here, trace_block, block_count, 0, row_count)
    psf_flat = psf_blocks.reshape(table_count * bin_count, pixel_count)
    traces = select_dot(spread_by_kind(spec_values, kinds, table_count), psf_flat).astype(jnp.bfloat16)
    slot_parts = jnp.stack([trace_slot // 256, trace_slot % 256], axis=1).astype(jnp.bfloat16)
    code_rows = -(-2 * capacity // pixel_count)
    places = [one_hot_rows(dest - step * capacity, capacity) for step in range(tile_count)]
    send = []
    for step in range(tile_count):
        codes = select_dot_t(slot_parts, places[step]).astype(jnp.bfloat16).reshape(2 * capacity)
        codes = jnp.pad(codes, (0, code_rows * pixel_count - 2 * capacity))
        block = select_dot_t(places[step], traces).astype(jnp.bfloat16)
        send.append(jnp.concatenate([block, codes.reshape(code_rows, pixel_count)], axis=0))
    got = exchange(send, "tile", 1)
    got_traces = [block[:capacity] for block in got]
    got_slots = []
    for block in got:
        codes = block[capacity:].reshape(code_rows * pixel_count)[: 2 * capacity]
        codes = codes.astype(jnp.int32).reshape(2, capacity)
        got_slots.append(codes[0] * 256 + codes[1])

    at_slot = [one_hot_rows(slots, slot_count) for slots in got_slots]
    partial_value = sum(select_dot_t(a, b) for a, b in zip(at_slot, got_traces))
    model_image = swap_add(partial_value, "band")
    residual = (
        bad_mask[0].astype(jnp.float32) * (model_image - observed[0].astype(jnp.float32))
    ).astype(jnp.bfloat16)

    under_rows = [select_dot(a, residual).astype(jnp.bfloat16) for a in at_slot]
    returned = exchange(under_rows, "tile", -1)
    entry_rows = sum(select_dot(p, r) for p, r in zip(places, returned)).astype(jnp.bfloat16)
    back_table = psf_blocks.transpose(0, 2, 1).reshape(table_count * pixel_count, bin_count)
    terms = select_dot(spread_by_kind(entry_rows, kinds, table_count), back_table)
    terms = terms.astype(jnp.bfloat16)

    if dither_count == 2:
        dither = lax.axis_index("dither")
        half_rows = row_count // 2
        own_start = dither * half_rows
        their_rows = row_hot(source_here, trace_block, block_count, half_rows - own_start, half_rows)
        own_rows = row_hot(source_here, trace_block, block_count, own_start, half_rows)
        theirs = select_dot_t(their_rows, terms).reshape(source_count // 2, block_count * bin_count)
        sent = lax.ppermute(theirs.astype(jnp.bfloat16), "dither", [(0, 1), (1, 0)])
        mine = select_dot_t(own_rows, terms).reshape(source_count // 2, block_count * bin_count)
        gradient = mine + sent.astype(jnp.float32)
    else:
        local_grad = select_dot_t(gather_spec, terms)
        local_grad = local_grad.reshape(source_count, block_count * bin_count)
        gradient = lax.psum_scatter(local_grad, "dither", scatter_dimension=0, tiled=True)
    return (gradient, residual[None])


def solution(mesh):
    in_specs = (
        P(("groups", "tile"), "band"),
        P(),
        P(("groups", "dither"), "tile", None),
        P(("groups", "dither"), "tile", None),
        P(("groups", "tile", "dither", "band"), None),
        P(("groups", "tile", "dither", "band")),
        P(("groups", "tile", "dither", "band"), None),
        P(("groups", "tile", "dither", "band")),
        P(("groups", "tile", "dither", "band")),
    )
    out_specs = (P(("groups", "tile", "dither"), "band"), P(("groups", "dither"), "tile", None))
    return jax.shard_map(
        per_device, mesh=mesh, in_specs=in_specs, out_specs=out_specs, check_vma=False
    )
```

```python
import functools

import jax
import jax.numpy as jnp
from jax import lax
from jax.sharding import PartitionSpec as P


def one_hot_rows(index, width):
    return (index[:, None] == jnp.arange(width, dtype=jnp.int32)[None, :]).astype(jnp.bfloat16)


def row_hot(source, block, block_count, start, width):
    rows = start + jnp.arange(width, dtype=jnp.int32)[None, :]
    return (
        (rows // block_count == source[:, None]) & (rows % block_count == block[:, None])
    ).astype(jnp.bfloat16)


def select_dot(selector, values, precision=None):
    return jnp.dot(selector, values, preferred_element_type=jnp.float32, precision=precision)


def select_dot_t(selector, values, precision=None):
    return lax.dot_general(
        selector,
        values,
        (((0,), (0,)), ((), ())),
        preferred_element_type=jnp.float32,
        precision=precision,
    )


def spread_by_kind(values, kinds, table_count):
    chosen = kinds[:, None, None] == jnp.arange(table_count, dtype=jnp.int32)[None, :, None]
    spread = jnp.where(chosen, values[:, None, :], jnp.zeros((), values.dtype))
    return spread.reshape(values.shape[0], table_count * values.shape[1])


def swap_add(value, axis):
    count = lax.axis_size(axis)
    if count == 2:
        return value + lax.ppermute(value, axis, [(0, 1), (1, 0)])
    return lax.psum(value, axis)


def exchange(blocks, axis, direction):
    count = lax.axis_size(axis)
    moved = [blocks[0]]
    for step in range(1, count):
        pairs = [(j, (j + direction * step) % count) for j in range(count)]
        moved.append(lax.ppermute(blocks[step], axis, pairs))
    return moved


def per_device(
    spectra,
    psf_blocks,
    observed,
    bad_mask,
    trace_tile,
    trace_slot,
    trace_source,
    trace_block,
    psf_index,
):
    tile_count = lax.axis_size("tile")
    dither_count = lax.axis_size("dither")
    entry_count = trace_slot.shape[0]
    capacity = 2 * entry_count // tile_count
    table_count, bin_count, pixel_count = psf_blocks.shape
    source_count = spectra.shape[0]
    block_count = spectra.shape[1] // bin_count
    row_count = source_count * block_count
    slot_count = observed.shape[1]
    send_count = tile_count * capacity

    target = trace_tile[:, 0]
    kinds = psf_index
    source_here = trace_source[:, 0]
    member = one_hot_rows(target, tile_count)
    entry_ids = jnp.arange(entry_count, dtype=jnp.int32)
    up_to = (entry_ids[None, :] <= entry_ids[:, None]).astype(jnp.bfloat16)
    running = select_dot(up_to, member)
    position = jnp.sum((running - 1.0) * member.astype(jnp.float32), axis=1).astype(jnp.int32)
    shift = (target - lax.axis_index("tile")) % tile_count
    dest = shift * capacity + position

    gather_spec = row_hot(source_here, trace_block, block_count, 0, row_count)
    spec_parts = [
        select_dot(
            ((source_here[:, None] == jnp.arange(source_count, dtype=jnp.int32)[None, :])
             & (trace_block[:, None] == part)).astype(jnp.bfloat16),
            spectra[:, part * bin_count : (part + 1) * bin_count],
        )
        for part in range(block_count)
    ]
    spec_values = functools.reduce(jnp.add, spec_parts).astype(jnp.bfloat16)
    psf_flat = psf_blocks.reshape(table_count * bin_count, pixel_count)
    traces = select_dot(spread_by_kind(spec_values, kinds, table_count), psf_flat).astype(jnp.bfloat16)
    slot_parts = jnp.stack([trace_slot // 256, trace_slot % 256], axis=1).astype(jnp.bfloat16)
    code_rows = -(-2 * capacity // pixel_count)
    places = [one_hot_rows(dest - step * capacity, capacity) for step in range(tile_count)]
    send = []
    for step in range(tile_count):
        codes = select_dot_t(slot_parts, places[step]).astype(jnp.bfloat16).reshape(2 * capacity)
        codes = jnp.pad(codes, (0, code_rows * pixel_count - 2 * capacity))
        block = select_dot_t(places[step], traces).astype(jnp.bfloat16)
        send.append(jnp.concatenate([block, codes.reshape(code_rows, pixel_count)], axis=0))
    got = exchange(send, "tile", 1)
    got_traces = [block[:capacity] for block in got]
    got_slots = []
    for block in got:
        codes = block[capacity:].reshape(code_rows * pixel_count)[: 2 * capacity]
        codes = codes.astype(jnp.int32).reshape(2, capacity)
        got_slots.append(codes[0] * 256 + codes[1])

    at_slot = [one_hot_rows(slots, slot_count) for slots in got_slots]
    partial_value = sum(select_dot_t(a, b) for a, b in zip(at_slot, got_traces))
    model_image = swap_add(partial_value, "band")
    residual = (
        bad_mask[0].astype(jnp.float32) * (model_image - observed[0].astype(jnp.float32))
    ).astype(jnp.bfloat16)

    under_rows = [select_dot(a, residual).astype(jnp.bfloat16) for a in at_slot]
    returned = exchange(under_rows, "tile", -1)
    entry_rows = sum(select_dot(p, r) for p, r in zip(places, returned)).astype(jnp.bfloat16)
    back_table = psf_blocks.transpose(0, 2, 1).reshape(table_count * pixel_count, bin_count)
    terms = select_dot(spread_by_kind(entry_rows, kinds, table_count), back_table)
    terms = terms.astype(jnp.bfloat16)

    if dither_count == 2:
        dither = lax.axis_index("dither")
        half_rows = row_count // 2
        own_start = dither * half_rows
        their_rows = row_hot(source_here, trace_block, block_count, half_rows - own_start, half_rows)
        own_rows = row_hot(source_here, trace_block, block_count, own_start, half_rows)
        theirs = select_dot_t(their_rows, terms).reshape(source_count // 2, block_count * bin_count)
        sent = lax.ppermute(theirs.astype(jnp.bfloat16), "dither", [(0, 1), (1, 0)])
        mine = select_dot_t(own_rows, terms).reshape(source_count // 2, block_count * bin_count)
        gradient = mine + sent.astype(jnp.float32)
    else:
        local_grad = select_dot_t(gather_spec, terms)
        local_grad = local_grad.reshape(source_count, block_count * bin_count)
        gradient = lax.psum_scatter(local_grad, "dither", scatter_dimension=0, tiled=True)
    return (gradient, residual[None])


def solution(mesh):
    in_specs = (
        P(("groups", "tile"), "band"),
        P(),
        P(("groups", "dither"), "tile", None),
        P(("groups", "dither"), "tile", None),
        P(("groups", "tile", "dither", "band"), None),
        P(("groups", "tile", "dither", "band")),
        P(("groups", "tile", "dither", "band"), None),
        P(("groups", "tile", "dither", "band")),
        P(("groups", "tile", "dither", "band")),
    )
    out_specs = (P(("groups", "tile", "dither"), "band"), P(("groups", "dither"), "tile", None))
    return jax.shard_map(
        per_device, mesh=mesh, in_specs=in_specs, out_specs=out_specs, check_vma=False
    )
```

```python
import jax
import jax.numpy as jnp
from jax import lax
from jax.sharding import PartitionSpec as P


def one_hot_rows(index, width):
    return (index[:, None] == jnp.arange(width, dtype=jnp.int32)[None, :]).astype(jnp.bfloat16)


def row_hot(source, block, block_count, start, width):
    rows = start + jnp.arange(width, dtype=jnp.int32)[None, :]
    return (
        (rows // block_count == source[:, None]) & (rows % block_count == block[:, None])
    ).astype(jnp.bfloat16)


def select_dot(selector, values, precision=None):
    return jnp.dot(selector, values, preferred_element_type=jnp.float32, precision=precision)


def select_dot_t(selector, values, precision=None):
    return lax.dot_general(
        selector,
        values,
        (((0,), (0,)), ((), ())),
        preferred_element_type=jnp.float32,
        precision=precision,
    )


def spread_by_kind(values, kinds, table_count):
    chosen = kinds[:, None, None] == jnp.arange(table_count, dtype=jnp.int32)[None, :, None]
    spread = jnp.where(chosen, values[:, None, :], jnp.zeros((), values.dtype))
    return spread.reshape(values.shape[0], table_count * values.shape[1])


def swap_add(value, axis):
    count = lax.axis_size(axis)
    if count == 2:
        return value + lax.ppermute(value, axis, [(0, 1), (1, 0)])
    return lax.psum(value, axis)


def exchange(blocks, axis, direction):
    count = lax.axis_size(axis)
    moved = [blocks[0]]
    for step in range(1, count):
        pairs = [(j, (j + direction * step) % count) for j in range(count)]
        moved.append(lax.ppermute(blocks[step], axis, pairs))
    return moved


def per_device(
    spectra,
    psf_blocks,
    observed,
    bad_mask,
    trace_tile,
    trace_slot,
    trace_source,
    trace_block,
    psf_index,
):
    tile_count = lax.axis_size("tile")
    dither_count = lax.axis_size("dither")
    entry_count = trace_slot.shape[0]
    capacity = 2 * entry_count // tile_count
    table_count, bin_count, pixel_count = psf_blocks.shape
    source_count = spectra.shape[0]
    block_count = spectra.shape[1] // bin_count
    row_count = source_count * block_count
    slot_count = observed.shape[1]
    send_count = tile_count * capacity

    target = trace_tile[:, 0]
    kinds = psf_index
    source_here = trace_source[:, 0]
    member = one_hot_rows(target, tile_count)
    entry_ids = jnp.arange(entry_count, dtype=jnp.int32)
    up_to = (entry_ids[None, :] <= entry_ids[:, None]).astype(jnp.bfloat16)
    running = select_dot(up_to, member)
    position = jnp.sum((running - 1.0) * member.astype(jnp.float32), axis=1).astype(jnp.int32)
    shift = (target - lax.axis_index("tile")) % tile_count
    dest = shift * capacity + position

    gather_spec = row_hot(source_here, trace_block, block_count, 0, row_count)
    spec_values = select_dot(gather_spec, spectra.reshape(row_count, bin_count)).astype(jnp.bfloat16)
    psf_flat = psf_blocks.reshape(table_count * bin_count, pixel_count)
    traces = select_dot(spread_by_kind(spec_values, kinds, table_count), psf_flat).astype(jnp.bfloat16)
    slot_parts = jnp.stack([trace_slot // 256, trace_slot % 256], axis=1).astype(jnp.bfloat16)
    code_rows = -(-2 * capacity // pixel_count)
    places = [one_hot_rows(dest - step * capacity, capacity) for step in range(tile_count)]
    send = []
    for step in range(tile_count):
        codes = select_dot_t(slot_parts, places[step]).astype(jnp.bfloat16).reshape(2 * capacity)
        codes = jnp.pad(codes, (0, code_rows * pixel_count - 2 * capacity))
        block = select_dot_t(places[step], traces).astype(jnp.bfloat16)
        send.append(jnp.concatenate([block, codes.reshape(code_rows, pixel_count)], axis=0))
    got = exchange(send, "tile", 1)
    got_traces = [block[:capacity] for block in got]
    at_slot = []
    for block in got:
        codes = block[capacity:].reshape(code_rows * pixel_count)[: 2 * capacity]
        codes = codes.astype(jnp.int32).reshape(2, capacity)
        at_slot.append(row_hot(codes[0], codes[1], 256, 0, slot_count))

    partial_value = sum(select_dot_t(a, b) for a, b in zip(at_slot, got_traces))
    model_image = swap_add(partial_value, "band")
    residual = (
        bad_mask[0].astype(jnp.float32) * (model_image - observed[0].astype(jnp.float32))
    ).astype(jnp.bfloat16)

    under_rows = [select_dot(a, residual).astype(jnp.bfloat16) for a in at_slot]
    returned = exchange(under_rows, "tile", -1)
    entry_rows = sum(select_dot(p, r) for p, r in zip(places, returned)).astype(jnp.bfloat16)
    back_table = psf_blocks.transpose(0, 2, 1).reshape(table_count * pixel_count, bin_count)
    terms = select_dot(spread_by_kind(entry_rows, kinds, table_count), back_table)
    terms = terms.astype(jnp.bfloat16)

    if dither_count == 2:
        dither = lax.axis_index("dither")
        half_rows = row_count // 2
        own_start = dither * half_rows
        their_rows = row_hot(source_here, trace_block, block_count, half_rows - own_start, half_rows)
        own_rows = row_hot(source_here, trace_block, block_count, own_start, half_rows)
        theirs = select_dot_t(their_rows, terms).reshape(source_count // 2, block_count * bin_count)
        sent = lax.ppermute(theirs.astype(jnp.bfloat16), "dither", [(0, 1), (1, 0)])
        mine = select_dot_t(own_rows, terms).reshape(source_count // 2, block_count * bin_count)
        gradient = mine + sent.astype(jnp.float32)
    else:
        local_grad = select_dot_t(gather_spec, terms)
        local_grad = local_grad.reshape(source_count, block_count * bin_count)
        gradient = lax.psum_scatter(local_grad, "dither", scatter_dimension=0, tiled=True)
    return (gradient, residual[None])


def solution(mesh):
    in_specs = (
        P(("groups", "tile"), "band"),
        P(),
        P(("groups", "dither"), "tile", None),
        P(("groups", "dither"), "tile", None),
        P(("groups", "tile", "dither", "band"), None),
        P(("groups", "tile", "dither", "band")),
        P(("groups", "tile", "dither", "band"), None),
        P(("groups", "tile", "dither", "band")),
        P(("groups", "tile", "dither", "band")),
    )
    out_specs = (P(("groups", "tile", "dither"), "band"), P(("groups", "dither"), "tile", None))
    return jax.shard_map(
        per_device, mesh=mesh, in_specs=in_specs, out_specs=out_specs, check_vma=False
    )
```
